256 devices in a mesh: gx: 64 (over y_hi, x, z), gy: 4 (over y_lo, core).
Axes of the slice: x: 4, y: 4 (y_hi: 2, y_lo: 2; y = y_hi * 2 + y_lo), z: 8, core: 2. Of those that a mesh axis runs over, the one named last changes fastest.
Arguments:
- base_flow: float32 [3, 1536, 32, 1024], P(None, 'gx', None, 'gy'), may hold values from -6 to 6
- adjoint: float32 [3, 1536, 32, 1024], P(None, 'gx', None, 'gy'), may hold values from -6 to 6
- first_op: bfloat16 [1024, 1024], replicated, may hold values from -2 to 2
- second_op: bfloat16 [1024, 1024], replicated, may hold values from -9 to 5
Outputs:
- new_adjoint: float32 [3, 1536, 32, 1024], P(None, 'gx', None, 'gy')
The draws below stay inside these ranges and needn't reach their ends.
All inputs are finite; a program needn't handle non-finite values.
Results may differ from the reference program's by a relative error of at most 0.0025.
Values may be sent and summed in bfloat16 or wider, within the bound.
No kernel may reach another device: no remote copies, remote signals or barrier semaphores. Data moves between devices by JAX's collectives and lax.ppermute only.
A program may use at most 128 MiB of HBM per device.

```python
import jax
import jax.numpy as jnp
from jax import lax

NY = 1024
NZ = 32
NX = 1536


def grid_metric(key):
    metric_key = jax.random.fold_in(key, 7)
    return jnp.exp(jax.random.uniform(metric_key, (NY, 1), jnp.float32, -0.7, 0.7))


def operator_jitter(key, salt):
    jitter_key = jax.random.fold_in(key, salt)
    jitter = jnp.clip(jax.random.normal(jitter_key, (NY, NY), jnp.float32), -4.0, 4.0)
    return 0.3 * jitter / jnp.sqrt(jnp.float32(NY))


def draw_first_op(key, part):
    row_index = jnp.arange(NY)[:, None]
    col_index = jnp.arange(NY)[None, :]
    distance = jnp.abs(col_index - row_index).astype(jnp.float32)
    signed = jnp.sign(col_index - row_index).astype(jnp.float32)
    banded = signed * 0.8 * jnp.power(jnp.float32(0.3), distance - 1.0)
    metric = grid_metric(key)
    return (metric * (banded + operator_jitter(key, 1))).astype(jnp.bfloat16)


def draw_second_op(key, part):
    row_index = jnp.arange(NY)[:, None]
    col_index = jnp.arange(NY)[None, :]
    distance = jnp.abs(col_index - row_index).astype(jnp.float32)
    banded = jnp.where(distance == 0.0, -2.0, jnp.power(jnp.float32(0.35), jnp.maximum(distance - 1.0, 0.0)))
    metric = grid_metric(key)
    return (metric * metric * (banded + operator_jitter(key, 2))).astype(jnp.bfloat16)


def level_of(rng, dims, shards, low, largest):
    factor_of = 1.0
    for axis_at, shards_of in shards:
        steps = jax.random.uniform(jax.random.fold_in(jax.random.fold_in(rng, 6), axis_at), (shards_of,), jnp.float32, low / len(shards), largest / len(shards))
        factor_of = factor_of * jnp.repeat(jnp.exp(steps), dims[axis_at] // shards_of).reshape((-1,) + (1,) * (len(dims) - 1 - axis_at))
    return factor_of


def gaussian(key, shape, deviation, bound, split=(), kind=jnp.bfloat16):
    values = jax.random.normal(key, shape, jnp.float32) * deviation
    if len(split) > 0:
        values = level_of(key, shape, split, -0.22, 0.18) * values
    return jnp.clip(values, min=-bound, max=bound).astype(kind)


def setup_inputs(seed: int = 0) -> dict:
    streams_of = jax.random.split(jax.random.key(seed), 5)
    base_flow = gaussian(streams_of[0], (3, NX, NZ, NY), 1.0, 6.0, ((1, 64), (3, 4)), jnp.float32)
    adjoint = gaussian(streams_of[1], (3, NX, NZ, NY), 1.0, 6.0, ((1, 64), (3, 4)), jnp.float32)
    first_op = draw_first_op(jax.random.fold_in(streams_of[4], 71), 0)
    second_op = draw_second_op(jax.random.fold_in(streams_of[4], 71), 0)
    return {"base_flow": base_flow, "adjoint": adjoint, "first_op": first_op, "second_op": second_op}


C_FIRST = (0.8, -0.2, 4.0 / 105.0, -1.0 / 280.0)
C_SECOND = (1.6, -0.2, 8.0 / 315.0, -1.0 / 560.0)
C_CENTER = -205.0 / 72.0
VISCOSITY = 0.1
STEP_WEIGHT = 0.5


def first_periodic(field, direction):
    result = C_FIRST[0] * (jnp.roll(field, -1, direction) - jnp.roll(field, 1, direction))
    for offset in range(2, 5):
        result = result + C_FIRST[offset - 1] * (jnp.roll(field, -offset, direction) - jnp.roll(field, offset, direction))
    return result


def second_periodic(field, direction):
    result = C_CENTER * field
    for offset in range(1, 5):
        result = result + C_SECOND[offset - 1] * (jnp.roll(field, -offset, direction) + jnp.roll(field, offset, direction))
    return result


def wall_operator(values, matrix):
    return jnp.einsum("fxzk,ik->fxzi", values.astype(jnp.float32), matrix.astype(jnp.float32), precision=lax.Precision.HIGHEST)


def wall_combine(normal_vel, slope_adj, curvature, adjoint_low, slope_base):
    wall_part = normal_vel[None] * slope_adj + VISCOSITY * curvature
    coupling = jnp.sum(adjoint_low * slope_base, axis=0)
    return wall_part.at[1].add(-coupling)


def reference(base_flow, adjoint, first_op, second_op):
    base_low = lax.optimization_barrier(base_flow.astype(jnp.bfloat16))
    adjoint_low = lax.optimization_barrier(adjoint.astype(jnp.bfloat16))
    wall_base = wall_operator(base_low, first_op)
    wall_adjoint = wall_operator(adjoint_low, first_op)
    wall_curv = wall_operator(adjoint_low, second_op)
    wall_part = wall_combine(base_low[1].astype(jnp.float32), wall_adjoint, wall_curv, adjoint_low.astype(jnp.float32), wall_base)
    dx_base = first_periodic(base_flow, 1)
    dz_base = first_periodic(base_flow, 2)
    dx_adj = first_periodic(adjoint, 1)
    dz_adj = first_periodic(adjoint, 2)
    dxx_adj = second_periodic(adjoint, 1)
    dzz_adj = second_periodic(adjoint, 2)
    tendency = base_flow[0][None] * dx_adj + base_flow[2][None] * dz_adj + VISCOSITY * (dxx_adj + dzz_adj) + wall_part
    tendency = tendency.at[0].add(-jnp.sum(adjoint * dx_base, axis=0))
    tendency = tendency.at[2].add(-jnp.sum(adjoint * dz_base, axis=0))
    updated = adjoint + STEP_WEIGHT * tendency
    wall_index = jnp.arange(NY, dtype=jnp.int32)
    interior = (wall_index > 0) & (wall_index < NY - 1)
    return jnp.where(interior, updated, jnp.float32(0.0))
```

```python
import jax
import jax.numpy as jnp
from jax import lax
from jax.sharding import PartitionSpec as P

C_FIRST = (0.8, -0.2, 4.0 / 105.0, -1.0 / 280.0)
C_SECOND = (1.6, -0.2, 8.0 / 315.0, -1.0 / 560.0)
C_CENTER = -205.0 / 72.0
VISCOSITY = 0.1
STEP_WEIGHT = 0.5
HALO = 4


def ring_shift(value, axis, forward):
    count = lax.axis_size(axis)
    if forward:
        pairs = [(i, (i + 1) % count) for i in range(count)]
    else:
        pairs = [((i + 1) % count, i) for i in range(count)]
    return lax.ppermute(value, axis, pairs)


def first_streamwise(extended, cells):
    result = C_FIRST[0] * (extended[:, HALO + 1 : HALO + 1 + cells] - extended[:, HALO - 1 : HALO - 1 + cells])
    for offset in range(2, 5):
        result = result + C_FIRST[offset - 1] * (
            extended[:, HALO + offset : HALO + offset + cells]
            - extended[:, HALO - offset : HALO - offset + cells]
        )
    return result


def second_streamwise(extended, cells):
    result = C_CENTER * extended[:, HALO : HALO + cells]
    for offset in range(1, 5):
        result = result + C_SECOND[offset - 1] * (
            extended[:, HALO + offset : HALO + offset + cells]
            + extended[:, HALO - offset : HALO - offset + cells]
        )
    return result


def first_periodic(field, direction):
    result = C_FIRST[0] * (jnp.roll(field, -1, direction) - jnp.roll(field, 1, direction))
    for offset in range(2, 5):
        result = result + C_FIRST[offset - 1] * (
            jnp.roll(field, -offset, direction) - jnp.roll(field, offset, direction)
        )
    return result


def second_periodic(field, direction):
    result = C_CENTER * field
    for offset in range(1, 5):
        result = result + C_SECOND[offset - 1] * (
            jnp.roll(field, -offset, direction) + jnp.roll(field, offset, direction)
        )
    return result


def body(base_flow, adjoint, first_op, second_op):
    comps, cells, spanwise, local_rows = base_flow.shape
    groups = lax.axis_size("gy")
    total_rows = local_rows * groups
    part = spanwise // groups

    tails = ring_shift(jnp.stack((base_flow[:, cells - HALO :], adjoint[:, cells - HALO :]), 0), "gx", True)
    heads = ring_shift(jnp.stack((base_flow[:, :HALO], adjoint[:, :HALO]), 0), "gx", False)

    base_low = lax.optimization_barrier(base_flow.astype(jnp.bfloat16))
    adjoint_low = lax.optimization_barrier(adjoint.astype(jnp.bfloat16))
    low = jnp.concatenate((base_low, adjoint_low), 0).reshape(2 * comps, cells, spanwise, 1, local_rows)
    lines = lax.all_to_all(low, "gy", split_axis=2, concat_axis=3, tiled=True)
    lines = lines.reshape(2 * comps, cells, part, total_rows)
    base_lines = lines[:comps]
    adj_lines = lines[comps:]
    slope_base = jnp.einsum("fxzk,ik->fxzi", base_lines, first_op, preferred_element_type=jnp.float32)
    slope_adj = jnp.einsum("fxzk,ik->fxzi", adj_lines, first_op, preferred_element_type=jnp.float32)
    curves = jnp.einsum("fxzk,ik->fxzi", adj_lines, second_op, preferred_element_type=jnp.float32)
    normal_vel = base_lines[1].astype(jnp.float32)
    coupling = jnp.sum(adj_lines.astype(jnp.float32) * slope_base, axis=0)
    wall_part = normal_vel[None] * slope_adj + VISCOSITY * curves
    wall_part = wall_part.at[1].add(-coupling)
    wall_part = wall_part.reshape(comps, cells, part, groups, local_rows)
    wall_part = lax.all_to_all(wall_part, "gy", split_axis=3, concat_axis=2, tiled=True)
    wall_part = wall_part.reshape(comps, cells, spanwise, local_rows)

    extended_base = jnp.concatenate((tails[0], base_flow, heads[0]), axis=1)
    extended_adj = jnp.concatenate((tails[1], adjoint, heads[1]), axis=1)
    dx_base = first_streamwise(extended_base, cells)
    dz_base = first_periodic(base_flow, 2)
    dx_adj = first_streamwise(extended_adj, cells)
    dxx_adj = second_streamwise(extended_adj, cells)
    dz_adj = first_periodic(adjoint, 2)
    dzz_adj = second_periodic(adjoint, 2)
    carried = (
        base_flow[0][None] * dx_adj + base_flow[2][None] * dz_adj + VISCOSITY * (dxx_adj + dzz_adj)
    )
    first_coupling = jnp.sum(adjoint * dx_base, axis=0)
    last_coupling = jnp.sum(adjoint * dz_base, axis=0)
    tendency = jnp.stack((carried[0] - first_coupling, carried[1], carried[2] - last_coupling), 0)
    updated = adjoint + STEP_WEIGHT * (tendency + wall_part)
    wall_index = lax.axis_index("gy") * local_rows + jnp.arange(local_rows, dtype=jnp.int32)
    interior = (wall_index > 0) & (wall_index < total_rows - 1)
    return jnp.where(interior, updated, jnp.float32(0.0))


def solution(mesh):
    return jax.shard_map(
        body,
        mesh=mesh,
        in_specs=(P(None, "gx", None, "gy"), P(None, "gx", None, "gy"), P(), P()),
        out_specs=P(None, "gx", None, "gy"),
        check_vma=False,
    )
```

```python
import jax
import jax.numpy as jnp
from jax import lax
from jax.sharding import PartitionSpec as P

C_FIRST = (0.8, -0.2, 4.0 / 105.0, -1.0 / 280.0)
C_SECOND = (1.6, -0.2, 8.0 / 315.0, -1.0 / 560.0)
C_CENTER = -205.0 / 72.0
VISCOSITY = 0.1
STEP_WEIGHT = 0.5
HALO = 4


def ring_shift(value, axis, forward):
    count = lax.axis_size(axis)
    if forward:
        pairs = [(i, (i + 1) % count) for i in range(count)]
    else:
        pairs = [((i + 1) % count, i) for i in range(count)]
    return lax.ppermute(value, axis, pairs)


def first_streamwise(extended, cells):
    result = C_FIRST[0] * (extended[:, HALO + 1 : HALO + 1 + cells] - extended[:, HALO - 1 : HALO - 1 + cells])
    for offset in range(2, 5):
        result = result + C_FIRST[offset - 1] * (
            extended[:, HALO + offset : HALO + offset + cells]
            - extended[:, HALO - offset : HALO - offset + cells]
        )
    return result


def second_streamwise(extended, cells):
    result = C_CENTER * extended[:, HALO : HALO + cells]
    for offset in range(1, 5):
        result = result + C_SECOND[offset - 1] * (
            extended[:, HALO + offset : HALO + offset + cells]
            + extended[:, HALO - offset : HALO - offset + cells]
        )
    return result


def first_periodic(field, direction):
    result = C_FIRST[0] * (jnp.roll(field, -1, direction) - jnp.roll(field, 1, direction))
    for offset in range(2, 5):
        result = result + C_FIRST[offset - 1] * (
            jnp.roll(field, -offset, direction) - jnp.roll(field, offset, direction)
        )
    return result


def second_periodic(field, direction):
    result = C_CENTER * field
    for offset in range(1, 5):
        result = result + C_SECOND[offset - 1] * (
            jnp.roll(field, -offset, direction) + jnp.roll(field, offset, direction)
        )
    return result


def body(base_flow, adjoint, first_op, second_op):
    comps, cells, spanwise, local_rows = base_flow.shape
    groups = lax.axis_size("gy")
    total_rows = local_rows * groups
    part = spanwise // groups

    tails = ring_shift(jnp.stack((base_flow[:, cells - HALO :], adjoint[:, cells - HALO :]), 0), "gx", True)
    heads = ring_shift(jnp.stack((base_flow[:, :HALO], adjoint[:, :HALO]), 0), "gx", False)

    base_low = lax.optimization_barrier(base_flow.astype(jnp.bfloat16))
    adjoint_low = lax.optimization_barrier(adjoint.astype(jnp.bfloat16))
    low = jnp.concatenate((base_low, adjoint_low), 0).reshape(2 * comps, cells, spanwise, 1, local_rows)
    lines = lax.all_to_all(low, "gy", split_axis=2, concat_axis=3, tiled=True)
    lines = lines.reshape(2 * comps, cells, part, total_rows)
    base_lines = lines[:comps]
    adj_lines = lines[comps:]
    slope_base = jnp.einsum("fxzk,ik->fxzi", base_lines, first_op, preferred_element_type=jnp.float32)
    slope_adj = jnp.einsum("fxzk,ik->fxzi", adj_lines, first_op, preferred_element_type=jnp.float32)
    curves = jnp.einsum("fxzk,ik->fxzi", adj_lines, second_op, preferred_element_type=jnp.float32)
    normal_vel = base_lines[1].astype(jnp.float32)
    coupling = jnp.sum(adj_lines.astype(jnp.float32) * slope_base, axis=0)
    wall_part = normal_vel[None] * slope_adj + VISCOSITY * curves
    wall_part = wall_part.at[1].add(-coupling)
    wall_part = wall_part.astype(jnp.bfloat16).reshape(comps, cells, part, groups, local_rows)
    wall_part = lax.all_to_all(wall_part, "gy", split_axis=3, concat_axis=2, tiled=True)
    wall_part = wall_part.reshape(comps, cells, spanwise, local_rows).astype(jnp.float32)

    extended_base = jnp.concatenate((tails[0], base_flow, heads[0]), axis=1)
    extended_adj = jnp.concatenate((tails[1], adjoint, heads[1]), axis=1)
    dx_base = first_streamwise(extended_base, cells)
    dz_base = first_periodic(base_flow, 2)
    dx_adj = first_streamwise(extended_adj, cells)
    dxx_adj = second_streamwise(extended_adj, cells)
    dz_adj = first_periodic(adjoint, 2)
    dzz_adj = second_periodic(adjoint, 2)
    carried = (
        base_flow[0][None] * dx_adj + base_flow[2][None] * dz_adj + VISCOSITY * (dxx_adj + dzz_adj)
    )
    first_coupling = jnp.sum(adjoint * dx_base, axis=0)
    last_coupling = jnp.sum(adjoint * dz_base, axis=0)
    tendency = jnp.stack((carried[0] - first_coupling, carried[1], carried[2] - last_coupling), 0)
    updated = adjoint + STEP_WEIGHT * (tendency + wall_part)
    wall_index = lax.axis_index("gy") * local_rows + jnp.arange(local_rows, dtype=jnp.int32)
    interior = (wall_index > 0) & (wall_index < total_rows - 1)
    return jnp.where(interior, updated, jnp.float32(0.0))


def solution(mesh):
    return jax.shard_map(
        body,
        mesh=mesh,
        in_specs=(P(None, "gx", None, "gy"), P(None, "gx", None, "gy"), P(), P()),
        out_specs=P(None, "gx", None, "gy"),
        check_vma=False,
    )
```

```python
import jax
import jax.numpy as jnp
from jax import lax
from jax.experimental import pallas as pl
from jax.experimental.pallas import tpu as pltpu
from jax.sharding import PartitionSpec as P

C_FIRST = (0.8, -0.2, 4.0 / 105.0, -1.0 / 280.0)
C_SECOND = (1.6, -0.2, 8.0 / 315.0, -1.0 / 560.0)
C_CENTER = -205.0 / 72.0
VISCOSITY = 0.1
STEP_WEIGHT = 0.5
HALO = 4
LANES = 128


def ring_shift(value, axis, forward):
    count = lax.axis_size(axis)
    if forward:
        pairs = [(i, (i + 1) % count) for i in range(count)]
    else:
        pairs = [((i + 1) % count, i) for i in range(count)]
    return lax.ppermute(value, axis, pairs)


def stencil_kernel(base_ref, adj_ref, tail_ref, head_ref, out_ref, ext_ref):
    comps, cells, span, lanes = base_ref.shape
    ext_ref[0, :, HALO : HALO + cells] = base_ref[...]
    ext_ref[1, :, HALO : HALO + cells] = adj_ref[...]
    ext_ref[:, :, :HALO] = tail_ref[...]
    ext_ref[:, :, HALO + cells :] = head_ref[...]

    def zshift(v, k):
        return pltpu.roll(v, (span - k) % span, 0)

    def derivs(field, c, xi, second):
        center = ext_ref[field, c, xi]
        plus = [ext_ref[field, c, xi + k] for k in range(1, 5)]
        minus = [ext_ref[field, c, xi - k] for k in range(1, 5)]
        zp = [zshift(center, k) for k in range(1, 5)]
        zm = [zshift(center, span - k) for k in range(1, 5)]
        dx = C_FIRST[0] * (plus[0] - minus[0])
        dz = C_FIRST[0] * (zp[0] - zm[0])
        for k in range(1, 4):
            dx = dx + C_FIRST[k] * (plus[k] - minus[k])
            dz = dz + C_FIRST[k] * (zp[k] - zm[k])
        if not second:
            return center, dx, dz, None, None
        dxx = C_CENTER * center
        dzz = C_CENTER * center
        for k in range(4):
            dxx = dxx + C_SECOND[k] * (plus[k] + minus[k])
            dzz = dzz + C_SECOND[k] * (zp[k] + zm[k])
        return center, dx, dz, dxx, dzz

    def step(x, carry):
        xi = x + HALO
        base = [derivs(0, j, xi, False) for j in range(comps)]
        adj = [derivs(1, c, xi, True) for c in range(comps)]
        first_coupling = adj[0][0] * base[0][1] + adj[1][0] * base[1][1] + adj[2][0] * base[2][1]
        last_coupling = adj[0][0] * base[0][2] + adj[1][0] * base[1][2] + adj[2][0] * base[2][2]
        for c in range(comps):
            center, dx, dz, dxx, dzz = adj[c]
            tendency = base[0][0] * dx + base[2][0] * dz + VISCOSITY * (dxx + dzz)
            if c == 0:
                tendency = tendency - first_coupling
            elif c == comps - 1:
                tendency = tendency - last_coupling
            out_ref[c, x] = center + STEP_WEIGHT * tendency
        return carry

    lax.fori_loop(0, cells, step, 0)


def stencil_update(base_flow, adjoint, tails, heads):
    comps, cells, span, rows = base_flow.shape
    lanes = LANES if rows % LANES == 0 else rows
    field_spec = pl.BlockSpec((comps, cells, span, lanes), lambda j: (0, 0, 0, j))
    halo_spec = pl.BlockSpec((2, comps, HALO, span, lanes), lambda j: (0, 0, 0, 0, j))
    return pl.pallas_call(
        stencil_kernel,
        grid=(rows // lanes,),
        in_specs=[field_spec, field_spec, halo_spec, halo_spec],
        out_specs=field_spec,
        out_shape=jax.ShapeDtypeStruct(base_flow.shape, jnp.float32),
        scratch_shapes=[pltpu.VMEM((2, comps, cells + 2 * HALO, span, lanes), jnp.float32)],
    )(base_flow, adjoint, tails, heads)


def body(base_flow, adjoint, first_op, second_op):
    comps, cells, spanwise, local_rows = base_flow.shape
    groups = lax.axis_size("gy")
    total_rows = local_rows * groups
    part = spanwise // groups

    tails = ring_shift(jnp.stack((base_flow[:, cells - HALO :], adjoint[:, cells - HALO :]), 0), "gx", True)
    heads = ring_shift(jnp.stack((base_flow[:, :HALO], adjoint[:, :HALO]), 0), "gx", False)

    base_low = lax.optimization_barrier(base_flow.astype(jnp.bfloat16))
    adjoint_low = lax.optimization_barrier(adjoint.astype(jnp.bfloat16))
    low = jnp.concatenate((base_low, adjoint_low), 0).reshape(2 * comps, cells, spanwise, 1, local_rows)
    lines = lax.all_to_all(low, "gy", split_axis=2, concat_axis=3, tiled=True)
    lines = lines.reshape(2 * comps, cells, part, total_rows)
    base_lines = lines[:comps]
    adj_lines = lines[comps:]
    slope_base = jnp.einsum("fxzk,ik->fxzi", base_lines, first_op, preferred_element_type=jnp.float32)
    slope_adj = jnp.einsum("fxzk,ik->fxzi", adj_lines, first_op, preferred_element_type=jnp.float32)
    curves = jnp.einsum("fxzk,ik->fxzi", adj_lines, second_op, preferred_element_type=jnp.float32)
    normal_vel = base_lines[1].astype(jnp.float32)
    coupling = jnp.sum(adj_lines.astype(jnp.float32) * slope_base, axis=0)
    wall_part = normal_vel[None] * slope_adj + VISCOSITY * curves
    wall_part = wall_part.at[1].add(-coupling)
    wall_part = wall_part.astype(jnp.bfloat16).reshape(comps, cells, part, groups, local_rows)
    wall_part = lax.all_to_all(wall_part, "gy", split_axis=3, concat_axis=2, tiled=True)
    wall_part = wall_part.reshape(comps, cells, spanwise, local_rows).astype(jnp.float32)

    partial = stencil_update(base_flow, adjoint, tails, heads)
    updated = partial + STEP_WEIGHT * wall_part
    wall_index = lax.axis_index("gy") * local_rows + jnp.arange(local_rows, dtype=jnp.int32)
    interior = (wall_index > 0) & (wall_index < total_rows - 1)
    return jnp.where(interior, updated, jnp.float32(0.0))


def solution(mesh):
    return jax.shard_map(
        body,
        mesh=mesh,
        in_specs=(P(None, "gx", None, "gy"), P(None, "gx", None, "gy"), P(), P()),
        out_specs=P(None, "gx", None, "gy"),
        check_vma=False,
    )
```

```python
import jax
import jax.numpy as jnp
from jax import lax
from jax.experimental import pallas as pl
from jax.experimental.pallas import tpu as pltpu
from jax.sharding import PartitionSpec as P

C_FIRST = (0.8, -0.2, 4.0 / 105.0, -1.0 / 280.0)
C_SECOND = (1.6, -0.2, 8.0 / 315.0, -1.0 / 560.0)
C_CENTER = -205.0 / 72.0
VISCOSITY = 0.1
STEP_WEIGHT = 0.5
HALO = 4
LANES = 128


def ring_shift(value, axis, forward):
    count = lax.axis_size(axis)
    if forward:
        pairs = [(i, (i + 1) % count) for i in range(count)]
    else:
        pairs = [((i + 1) % count, i) for i in range(count)]
    return lax.ppermute(value, axis, pairs)


def stencil_kernel(base_ref, adj_ref, tail_ref, head_ref, *rest):
    out_ref, ext_ref = rest[-2:]
    comps, cells, span, lanes = base_ref.shape
    ext_ref[0, :, HALO : HALO + cells] = base_ref[...]
    ext_ref[1, :, HALO : HALO + cells] = adj_ref[...]
    ext_ref[:, :, :HALO] = tail_ref[...]
    ext_ref[:, :, HALO + cells :] = head_ref[...]

    def zshift(v, k):
        return pltpu.roll(v, (span - k) % span, 0)

    def derivs(field, c, xi, second):
        center = ext_ref[field, c, xi]
        plus = [ext_ref[field, c, xi + k] for k in range(1, 5)]
        minus = [ext_ref[field, c, xi - k] for k in range(1, 5)]
        zp = [zshift(center, k) for k in range(1, 5)]
        zm = [zshift(center, span - k) for k in range(1, 5)]
        dx = C_FIRST[0] * (plus[0] - minus[0])
        dz = C_FIRST[0] * (zp[0] - zm[0])
        for k in range(1, 4):
            dx = dx + C_FIRST[k] * (plus[k] - minus[k])
            dz = dz + C_FIRST[k] * (zp[k] - zm[k])
        if not second:
            return center, dx, dz, None, None
        dxx = C_CENTER * center
        dzz = C_CENTER * center
        for k in range(4):
            dxx = dxx + C_SECOND[k] * (plus[k] + minus[k])
            dzz = dzz + C_SECOND[k] * (zp[k] + zm[k])
        return center, dx, dz, dxx, dzz

    def step(x, carry):
        xi = x + HALO
        base = [derivs(0, j, xi, False) for j in range(comps)]
        adj = [derivs(1, c, xi, True) for c in range(comps)]
        first_coupling = adj[0][0] * base[0][1] + adj[1][0] * base[1][1] + adj[2][0] * base[2][1]
        last_coupling = adj[0][0] * base[0][2] + adj[1][0] * base[1][2] + adj[2][0] * base[2][2]
        for c in range(comps):
            center, dx, dz, dxx, dzz = adj[c]
            tendency = base[0][0] * dx + base[2][0] * dz + VISCOSITY * (dxx + dzz)
            if c == 0:
                tendency = tendency - first_coupling
            elif c == comps - 1:
                tendency = tendency - last_coupling
            out_ref[c, x] = center + STEP_WEIGHT * tendency
        return carry

    lax.fori_loop(0, cells, step, 0)


def stencil_update(base_flow, adjoint, tails, heads, block, previous=None):
    comps, cells, span, rows = base_flow.shape
    field_spec = pl.BlockSpec((comps, cells, span, LANES), lambda j: (0, 0, 0, block))
    halo_spec = pl.BlockSpec((2, comps, HALO, span, LANES), lambda j: (0, 0, 0, 0, block))
    in_specs = [field_spec, field_spec, halo_spec, halo_spec]
    operands = [base_flow, adjoint, tails, heads]
    aliases = {}
    if previous is not None:
        in_specs.append(pl.BlockSpec(memory_space=pl.ANY))
        operands.append(previous)
        aliases = {4: 0}
    return pl.pallas_call(
        stencil_kernel,
        grid=(1,),
        in_specs=in_specs,
        out_specs=field_spec,
        out_shape=jax.ShapeDtypeStruct(base_flow.shape, jnp.float32),
        scratch_shapes=[pltpu.VMEM((2, comps, cells + 2 * HALO, span, LANES), jnp.float32)],
        input_output_aliases=aliases,
    )(*operands)


def body(base_flow, adjoint, first_op, second_op):
    comps, cells, spanwise, local_rows = base_flow.shape
    groups = lax.axis_size("gy")
    total_rows = local_rows * groups
    part = spanwise // groups

    tails = ring_shift(jnp.stack((base_flow[:, cells - HALO :], adjoint[:, cells - HALO :]), 0), "gx", True)
    heads = ring_shift(jnp.stack((base_flow[:, :HALO], adjoint[:, :HALO]), 0), "gx", False)

    base_low = lax.optimization_barrier(base_flow.astype(jnp.bfloat16))
    adjoint_low = lax.optimization_barrier(adjoint.astype(jnp.bfloat16))
    low = jnp.concatenate((base_low, adjoint_low), 0).reshape(2 * comps, cells, spanwise, 1, local_rows)
    lines = lax.all_to_all(low, "gy", split_axis=2, concat_axis=3, tiled=True)
    partial = stencil_update(base_flow, adjoint, tails, heads, 0)
    lines, partial = lax.optimization_barrier((lines, partial))
    lines = lines.reshape(2 * comps, cells, part, total_rows)
    base_lines = lines[:comps]
    adj_lines = lines[comps:]
    slope_base = jnp.einsum("fxzk,ik->fxzi", base_lines, first_op, preferred_element_type=jnp.float32)
    slope_adj = jnp.einsum("fxzk,ik->fxzi", adj_lines, first_op, preferred_element_type=jnp.float32)
    curves = jnp.einsum("fxzk,ik->fxzi", adj_lines, second_op, preferred_element_type=jnp.float32)
    normal_vel = base_lines[1].astype(jnp.float32)
    coupling = jnp.sum(adj_lines.astype(jnp.float32) * slope_base, axis=0)
    wall_part = normal_vel[None] * slope_adj + VISCOSITY * curves
    wall_part = wall_part.at[1].add(-coupling)
    wall_part = wall_part.astype(jnp.bfloat16).reshape(comps, cells, part, groups, local_rows)
    wall_part, partial = lax.optimization_barrier((wall_part, partial))
    wall_part = lax.all_to_all(wall_part, "gy", split_axis=3, concat_axis=2, tiled=True)
    wall_part = wall_part.reshape(comps, cells, spanwise, local_rows).astype(jnp.float32)

    for block in range(1, local_rows // LANES):
        partial = stencil_update(base_flow, adjoint, tails, heads, block, partial)
    updated = partial + STEP_WEIGHT * wall_part
    wall_index = lax.axis_index("gy") * local_rows + jnp.arange(local_rows, dtype=jnp.int32)
    interior = (wall_index > 0) & (wall_index < total_rows - 1)
    return jnp.where(interior, updated, jnp.float32(0.0))


def solution(mesh):
    return jax.shard_map(
        body,
        mesh=mesh,
        in_specs=(P(None, "gx", None, "gy"), P(None, "gx", None, "gy"), P(), P()),
        out_specs=P(None, "gx", None, "gy"),
        check_vma=False,
    )
```

```python
import jax
import jax.numpy as jnp
from jax import lax
from jax.experimental import pallas as pl
from jax.experimental.pallas import tpu as pltpu
from jax.sharding import PartitionSpec as P

C_FIRST = (0.8, -0.2, 4.0 / 105.0, -1.0 / 280.0)
C_SECOND = (1.6, -0.2, 8.0 / 315.0, -1.0 / 560.0)
C_CENTER = -205.0 / 72.0
VISCOSITY = 0.1
STEP_WEIGHT = 0.5
HALO = 4
LANES = 128


def ring_shift(value, axis, forward):
    count = lax.axis_size(axis)
    if forward:
        pairs = [(i, (i + 1) % count) for i in range(count)]
    else:
        pairs = [((i + 1) % count, i) for i in range(count)]
    return lax.ppermute(value, axis, pairs)


def cell_update(load, x, write):
    span = load(0, 0, x).shape[0]

    def zshift(v, k):
        return pltpu.roll(v, (span - k) % span, 0)

    def derivs(field, c, second):
        center = load(field, c, x)
        plus = [load(field, c, x + k) for k in range(1, 5)]
        minus = [load(field, c, x - k) for k in range(1, 5)]
        zp = [zshift(center, k) for k in range(1, 5)]
        zm = [zshift(center, span - k) for k in range(1, 5)]
        dx = C_FIRST[0] * (plus[0] - minus[0])
        dz = C_FIRST[0] * (zp[0] - zm[0])
        for k in range(1, 4):
            dx = dx + C_FIRST[k] * (plus[k] - minus[k])
            dz = dz + C_FIRST[k] * (zp[k] - zm[k])
        if not second:
            return center, dx, dz, None, None
        dxx = C_CENTER * center
        dzz = C_CENTER * center
        for k in range(4):
            dxx = dxx + C_SECOND[k] * (plus[k] + minus[k])
            dzz = dzz + C_SECOND[k] * (zp[k] + zm[k])
        return center, dx, dz, dxx, dzz

    base = [derivs(0, j, False) for j in range(3)]
    adj = [derivs(1, c, True) for c in range(3)]
    first_coupling = adj[0][0] * base[0][1] + adj[1][0] * base[1][1] + adj[2][0] * base[2][1]
    last_coupling = adj[0][0] * base[0][2] + adj[1][0] * base[1][2] + adj[2][0] * base[2][2]
    for c in range(3):
        center, dx, dz, dxx, dzz = adj[c]
        tendency = base[0][0] * dx + base[2][0] * dz + VISCOSITY * (dxx + dzz)
        if c == 0:
            tendency = tendency - first_coupling
        elif c == 2:
            tendency = tendency - last_coupling
        write(c, center + STEP_WEIGHT * tendency)


def interior_kernel(base_ref, adj_ref, out_ref):
    first = (pl.program_id(1) + 1) * HALO

    def load(field, c, x):
        return (base_ref if field == 0 else adj_ref)[c, x]

    def step(i, carry):
        def write(c, value):
            out_ref[c, i] = value

        cell_update(load, first + i, write)
        return carry

    lax.fori_loop(0, HALO, step, 0)


def interior_update(base_flow, adjoint):
    comps, cells, span, rows = base_flow.shape
    field_spec = pl.BlockSpec((comps, cells, span, LANES), lambda j, b: (0, 0, 0, j))
    out_spec = pl.BlockSpec((comps, HALO, span, LANES), lambda j, b: (0, b + 1, 0, j))
    return pl.pallas_call(
        interior_kernel,
        grid=(rows // LANES, cells // HALO - 2),
        in_specs=[field_spec, field_spec],
        out_specs=out_spec,
        out_shape=jax.ShapeDtypeStruct(base_flow.shape, jnp.float32),
    )(base_flow, adjoint)


def boundary_kernel(base_ref, adj_ref, tail_ref, head_ref, prev_ref, out_ref, ext_ref):
    comps, cells, span, rows = base_ref.shape
    side = pl.program_id(0)

    @pl.when(side == 0)
    def _():
        ext_ref[0, :, HALO : HALO + cells] = base_ref[...]
        ext_ref[1, :, HALO : HALO + cells] = adj_ref[...]
        ext_ref[:, :, :HALO] = tail_ref[...]
        ext_ref[:, :, HALO + cells :] = head_ref[...]

    first = side * (cells - HALO)
    for lane in range(rows // LANES):
        lanes = pl.ds(lane * LANES, LANES)

        def load(field, c, x, lanes=lanes):
            return ext_ref[field, c, x + HALO, :, lanes]

        def step(i, carry, lanes=lanes, load=load):
            def write(c, value):
                out_ref[c, i, :, lanes] = value

            cell_update(load, first + i, write)
            return carry

        lax.fori_loop(0, HALO, step, 0)


def boundary_update(base_flow, adjoint, tails, heads, previous):
    comps, cells, span, rows = base_flow.shape
    full_spec = pl.BlockSpec((comps, cells, span, rows), lambda s: (0, 0, 0, 0))
    halo_spec = pl.BlockSpec((2, comps, HALO, span, rows), lambda s: (0, 0, 0, 0, 0))
    out_spec = pl.BlockSpec((comps, HALO, span, rows), lambda s: (0, s * (cells // HALO - 1), 0, 0))
    return pl.pallas_call(
        boundary_kernel,
        grid=(2,),
        in_specs=[full_spec, full_spec, halo_spec, halo_spec, pl.BlockSpec(memory_space=pl.ANY)],
        out_specs=out_spec,
        out_shape=jax.ShapeDtypeStruct(base_flow.shape, jnp.float32),
        scratch_shapes=[pltpu.VMEM((2, comps, cells + 2 * HALO, span, rows), jnp.float32)],
        input_output_aliases={4: 0},
    )(base_flow, adjoint, tails, heads, previous)


def body(base_flow, adjoint, first_op, second_op):
    comps, cells, spanwise, local_rows = base_flow.shape
    groups = lax.axis_size("gy")
    total_rows = local_rows * groups
    part = spanwise // groups

    base_low = lax.optimization_barrier(base_flow.astype(jnp.bfloat16))
    adjoint_low = lax.optimization_barrier(adjoint.astype(jnp.bfloat16))
    low = jnp.concatenate((base_low, adjoint_low), 0).reshape(2 * comps, cells, spanwise, 1, local_rows)
    lines = lax.all_to_all(low, "gy", split_axis=2, concat_axis=3, tiled=True)
    partial = interior_update(base_flow, adjoint)
    tail_cells = jnp.stack((base_flow[:, cells - HALO :], adjoint[:, cells - HALO :]), 0)
    head_cells = jnp.stack((base_flow[:, :HALO], adjoint[:, :HALO]), 0)
    lines, partial, tail_cells, head_cells = lax.optimization_barrier((lines, partial, tail_cells, head_cells))
    tails = ring_shift(tail_cells, "gx", True)
    heads = ring_shift(head_cells, "gx", False)
    lines = lines.reshape(2 * comps, cells, part, total_rows)
    base_lines = lines[:comps]
    adj_lines = lines[comps:]
    slope_base = jnp.einsum("fxzk,ik->fxzi", base_lines, first_op, preferred_element_type=jnp.float32)
    slope_adj = jnp.einsum("fxzk,ik->fxzi", adj_lines, first_op, preferred_element_type=jnp.float32)
    curves = jnp.einsum("fxzk,ik->fxzi", adj_lines, second_op, preferred_element_type=jnp.float32)
    normal_vel = base_lines[1].astype(jnp.float32)
    coupling = jnp.sum(adj_lines.astype(jnp.float32) * slope_base, axis=0)
    wall_part = normal_vel[None] * slope_adj + VISCOSITY * curves
    wall_part = wall_part.at[1].add(-coupling)
    wall_part = wall_part.astype(jnp.bfloat16).reshape(comps, cells, part, groups, local_rows)
    wall_part, partial = lax.optimization_barrier((wall_part, partial))
    wall_part = lax.all_to_all(wall_part, "gy", split_axis=3, concat_axis=2, tiled=True)
    wall_part = wall_part.reshape(comps, cells, spanwise, local_rows).astype(jnp.float32)

    partial = boundary_update(base_flow, adjoint, tails, heads, partial)
    updated = partial + STEP_WEIGHT * wall_part
    wall_index = lax.axis_index("gy") * local_rows + jnp.arange(local_rows, dtype=jnp.int32)
    interior = (wall_index > 0) & (wall_index < total_rows - 1)
    return jnp.where(interior, updated, jnp.float32(0.0))


def solution(mesh):
    return jax.shard_map(
        body,
        mesh=mesh,
        in_specs=(P(None, "gx", None, "gy"), P(None, "gx", None, "gy"), P(), P()),
        out_specs=P(None, "gx", None, "gy"),
        check_vma=False,
    )
```

```python
import jax
import jax.numpy as jnp
from jax import lax
from jax.experimental import pallas as pl
from jax.experimental.pallas import tpu as pltpu
from jax.sharding import PartitionSpec as P

C_FIRST = (0.8, -0.2, 4.0 / 105.0, -1.0 / 280.0)
C_SECOND = (1.6, -0.2, 8.0 / 315.0, -1.0 / 560.0)
C_CENTER = -205.0 / 72.0
VISCOSITY = 0.1
STEP_WEIGHT = 0.5
HALO = 4
LANES = 128


def ring_shift(value, axis, forward):
    count = lax.axis_size(axis)
    if forward:
        pairs = [(i, (i + 1) % count) for i in range(count)]
    else:
        pairs = [((i + 1) % count, i) for i in range(count)]
    return lax.ppermute(value, axis, pairs)


def cell_update(load, x, write):
    span = load(0, 0, x).shape[0]

    def zshift(v, k):
        return pltpu.roll(v, (span - k) % span, 0)

    def derivs(field, c, second):
        center = load(field, c, x)
        plus = [load(field, c, x + k) for k in range(1, 5)]
        minus = [load(field, c, x - k) for k in range(1, 5)]
        zp = [zshift(center, k) for k in range(1, 5)]
        zm = [zshift(center, span - k) for k in range(1, 5)]
        dx = C_FIRST[0] * (plus[0] - minus[0])
        dz = C_FIRST[0] * (zp[0] - zm[0])
        for k in range(1, 4):
            dx = dx + C_FIRST[k] * (plus[k] - minus[k])
            dz = dz + C_FIRST[k] * (zp[k] - zm[k])
        if not second:
            return center, dx, dz, None, None
        dxx = C_CENTER * center
        dzz = C_CENTER * center
        for k in range(4):
            dxx = dxx + C_SECOND[k] * (plus[k] + minus[k])
            dzz = dzz + C_SECOND[k] * (zp[k] + zm[k])
        return center, dx, dz, dxx, dzz

    base = [derivs(0, j, False) for j in range(3)]
    adj = [derivs(1, c, True) for c in range(3)]
    first_coupling = adj[0][0] * base[0][1] + adj[1][0] * base[1][1] + adj[2][0] * base[2][1]
    last_coupling = adj[0][0] * base[0][2] + adj[1][0] * base[1][2] + adj[2][0] * base[2][2]
    for c in range(3):
        center, dx, dz, dxx, dzz = adj[c]
        tendency = base[0][0] * dx + base[2][0] * dz + VISCOSITY * (dxx + dzz)
        if c == 0:
            tendency = tendency - first_coupling
        elif c == 2:
            tendency = tendency - last_coupling
        write(c, center + STEP_WEIGHT * tendency)


def interior_kernel(base_ref, adj_ref, out_ref):
    first = (pl.program_id(1) + 1) * HALO

    def load(field, c, x):
        return (base_ref if field == 0 else adj_ref)[c, x]

    def step(i, carry):
        def write(c, value):
            out_ref[c, i] = value

        cell_update(load, first + i, write)
        return carry

    lax.fori_loop(0, HALO, step, 0)


def interior_update(base_flow, adjoint):
    comps, cells, span, rows = base_flow.shape
    field_spec = pl.BlockSpec((comps, cells, span, LANES), lambda j, b: (0, 0, 0, j))
    out_spec = pl.BlockSpec((comps, HALO, span, LANES), lambda j, b: (0, b + 1, 0, j))
    return pl.pallas_call(
        interior_kernel,
        grid=(rows // LANES, cells // HALO - 2),
        in_specs=[field_spec, field_spec],
        out_specs=out_spec,
        out_shape=jax.ShapeDtypeStruct(base_flow.shape, jnp.float32),
    )(base_flow, adjoint)


def boundary_kernel(base_ref, adj_ref, tail_ref, head_ref, prev_ref, out_ref, ext_ref):
    comps, cells, span, rows = base_ref.shape
    side = pl.program_id(0)

    @pl.when(side == 0)
    def _():
        ext_ref[0, :, HALO : HALO + cells] = base_ref[...]
        ext_ref[1, :, HALO : HALO + cells] = adj_ref[...]
        ext_ref[:, :, :HALO] = tail_ref[...]
        ext_ref[:, :, HALO + cells :] = head_ref[...]

    first = side * (cells - HALO)
    for lane in range(rows // LANES):
        lanes = pl.ds(lane * LANES, LANES)

        def load(field, c, x, lanes=lanes):
            return ext_ref[field, c, x + HALO, :, lanes]

        def step(i, carry, lanes=lanes, load=load):
            def write(c, value):
                out_ref[c, i, :, lanes] = value

            cell_update(load, first + i, write)
            return carry

        lax.fori_loop(0, HALO, step, 0)


def boundary_update(base_flow, adjoint, tails, heads, previous):
    comps, cells, span, rows = base_flow.shape
    full_spec = pl.BlockSpec((comps, cells, span, rows), lambda s: (0, 0, 0, 0))
    halo_spec = pl.BlockSpec((2, comps, HALO, span, rows), lambda s: (0, 0, 0, 0, 0))
    out_spec = pl.BlockSpec((comps, HALO, span, rows), lambda s: (0, s * (cells // HALO - 1), 0, 0))
    return pl.pallas_call(
        boundary_kernel,
        grid=(2,),
        in_specs=[full_spec, full_spec, halo_spec, halo_spec, pl.BlockSpec(memory_space=pl.ANY)],
        out_specs=out_spec,
        out_shape=jax.ShapeDtypeStruct(base_flow.shape, jnp.float32),
        scratch_shapes=[pltpu.VMEM((2, comps, cells + 2 * HALO, span, rows), jnp.float32)],
        input_output_aliases={4: 0},
    )(base_flow, adjoint, tails, heads, previous)


def body(base_flow, adjoint, first_op, second_op):
    comps, cells, spanwise, local_rows = base_flow.shape
    groups = lax.axis_size("gy")
    total_rows = local_rows * groups
    part = spanwise // groups

    base_low = base_flow.astype(jnp.bfloat16)
    adjoint_low = adjoint.astype(jnp.bfloat16)
    span_cells = cells // groups
    low = jnp.concatenate((base_low, adjoint_low), 0).reshape(2 * comps, groups, span_cells, spanwise, local_rows)
    low = jnp.transpose(low, (1, 0, 2, 3, 4))
    lines = lax.all_to_all(low, "gy", split_axis=0, concat_axis=0, tiled=True)
    partial = interior_update(base_flow, adjoint)
    tail_cells = jnp.stack((base_flow[:, cells - HALO :], adjoint[:, cells - HALO :]), 0)
    head_cells = jnp.stack((base_flow[:, :HALO], adjoint[:, :HALO]), 0)
    lines, partial, tail_cells, head_cells = lax.optimization_barrier((lines, partial, tail_cells, head_cells))
    tails = ring_shift(tail_cells, "gx", True)
    heads = ring_shift(head_cells, "gx", False)
    first_blocks = first_op.reshape(total_rows, groups, local_rows)
    second_blocks = second_op.reshape(total_rows, groups, local_rows)
    base_lines = lines[:, :comps]
    adj_lines = lines[:, comps:]
    slope_base = jnp.einsum("qfxzr,iqr->fxzi", base_lines, first_blocks, preferred_element_type=jnp.float32)
    slope_adj = jnp.einsum("qfxzr,iqr->fxzi", adj_lines, first_blocks, preferred_element_type=jnp.float32)
    curves = jnp.einsum("qfxzr,iqr->fxzi", adj_lines, second_blocks, preferred_element_type=jnp.float32)
    def to_lines(value):
        return jnp.transpose(value, (1, 2, 3, 0, 4)).reshape(value.shape[1], span_cells, spanwise, total_rows)
    normal_vel = to_lines(base_lines[:, 1:2])[0].astype(jnp.float32)
    coupling = jnp.sum(to_lines(adj_lines).astype(jnp.float32) * slope_base, axis=0)
    wall_part = normal_vel[None] * slope_adj + VISCOSITY * curves
    wall_part = wall_part.at[1].add(-coupling)
    wall_part = wall_part.astype(jnp.bfloat16).reshape(comps, span_cells, spanwise, groups, local_rows)
    wall_part = jnp.transpose(wall_part, (3, 0, 1, 2, 4))
    wall_part, partial = lax.optimization_barrier((wall_part, partial))
    wall_part = lax.all_to_all(wall_part, "gy", split_axis=0, concat_axis=0, tiled=True)
    wall_part = jnp.transpose(wall_part, (1, 0, 2, 3, 4)).reshape(comps, cells, spanwise, local_rows).astype(jnp.float32)

    partial = boundary_update(base_flow, adjoint, tails, heads, partial)
    updated = partial + STEP_WEIGHT * wall_part
    wall_index = lax.axis_index("gy") * local_rows + jnp.arange(local_rows, dtype=jnp.int32)
    interior = (wall_index > 0) & (wall_index < total_rows - 1)
    return jnp.where(interior, updated, jnp.float32(0.0))


def solution(mesh):
    return jax.shard_map(
        body,
        mesh=mesh,
        in_specs=(P(None, "gx", None, "gy"), P(None, "gx", None, "gy"), P(), P()),
        out_specs=P(None, "gx", None, "gy"),
        check_vma=False,
    )
```

```python
import functools

import jax
import jax.numpy as jnp
from jax import lax
from jax.experimental import pallas as pl
from jax.experimental.pallas import tpu as pltpu
from jax.sharding import PartitionSpec as P

C_FIRST = (0.8, -0.2, 4.0 / 105.0, -1.0 / 280.0)
C_SECOND = (1.6, -0.2, 8.0 / 315.0, -1.0 / 560.0)
C_CENTER = -205.0 / 72.0
VISCOSITY = 0.1
STEP_WEIGHT = 0.5
HALO = 4
LANES = 128


def ring_shift(value, axis, forward, far, want_far):
    count = lax.axis_size(axis)
    links = [i for i in range(count) if far[i] == want_far]
    if forward:
        pairs = [(i, (i + 1) % count) for i in links]
    else:
        pairs = [((i + 1) % count, i) for i in links]
    return lax.ppermute(value, axis, pairs)


def cell_update(load, x, write):
    span = load(0, 0, x).shape[0]

    def zshift(v, k):
        return pltpu.roll(v, (span - k) % span, 0)

    def derivs(field, c, second):
        center = load(field, c, x)
        plus = [load(field, c, x + k) for k in range(1, 5)]
        minus = [load(field, c, x - k) for k in range(1, 5)]
        zp = [zshift(center, k) for k in range(1, 5)]
        zm = [zshift(center, span - k) for k in range(1, 5)]
        dx = C_FIRST[0] * (plus[0] - minus[0])
        dz = C_FIRST[0] * (zp[0] - zm[0])
        for k in range(1, 4):
            dx = dx + C_FIRST[k] * (plus[k] - minus[k])
            dz = dz + C_FIRST[k] * (zp[k] - zm[k])
        if not second:
            return center, dx, dz, None, None
        dxx = C_CENTER * center
        dzz = C_CENTER * center
        for k in range(4):
            dxx = dxx + C_SECOND[k] * (plus[k] + minus[k])
            dzz = dzz + C_SECOND[k] * (zp[k] + zm[k])
        return center, dx, dz, dxx, dzz

    base = [derivs(0, j, False) for j in range(3)]
    adj = [derivs(1, c, True) for c in range(3)]
    first_coupling = adj[0][0] * base[0][1] + adj[1][0] * base[1][1] + adj[2][0] * base[2][1]
    last_coupling = adj[0][0] * base[0][2] + adj[1][0] * base[1][2] + adj[2][0] * base[2][2]
    for c in range(3):
        center, dx, dz, dxx, dzz = adj[c]
        tendency = base[0][0] * dx + base[2][0] * dz + VISCOSITY * (dxx + dzz)
        if c == 0:
            tendency = tendency - first_coupling
        elif c == 2:
            tendency = tendency - last_coupling
        write(c, center + STEP_WEIGHT * tendency)


def interior_kernel(base_ref, adj_ref, out_ref):
    first = (pl.program_id(1) + 1) * HALO

    def load(field, c, x):
        return (base_ref if field == 0 else adj_ref)[c, x]

    def step(i, carry):
        def write(c, value):
            out_ref[c, i] = value

        cell_update(load, first + i, write)
        return carry

    lax.fori_loop(0, HALO, step, 0)


def interior_update(base_flow, adjoint):
    comps, cells, span, rows = base_flow.shape
    field_spec = pl.BlockSpec((comps, cells, span, LANES), lambda j, b: (0, 0, 0, j))
    out_spec = pl.BlockSpec((comps, HALO, span, LANES), lambda j, b: (0, b + 1, 0, j))
    return pl.pallas_call(
        interior_kernel,
        grid=(rows // LANES, cells // HALO - 2),
        in_specs=[field_spec, field_spec],
        out_specs=out_spec,
        out_shape=jax.ShapeDtypeStruct(base_flow.shape, jnp.float32),
    )(base_flow, adjoint)


def boundary_kernel(base_ref, adj_ref, tail_ref, head_ref, far_tail_ref, far_head_ref, prev_ref, out_ref, ext_ref):
    comps, cells, span, rows = base_ref.shape
    side = pl.program_id(0)

    @pl.when(side == 0)
    def _():
        ext_ref[0, :, HALO : HALO + cells] = base_ref[...]
        ext_ref[1, :, HALO : HALO + cells] = adj_ref[...]
        ext_ref[:, :, :HALO] = tail_ref[...] + far_tail_ref[...]
        ext_ref[:, :, HALO + cells :] = head_ref[...] + far_head_ref[...]

    first = side * (cells - HALO)
    for lane in range(rows // LANES):
        lanes = pl.ds(lane * LANES, LANES)

        def load(field, c, x, lanes=lanes):
            return ext_ref[field, c, x + HALO, :, lanes]

        def step(i, carry, lanes=lanes, load=load):
            def write(c, value):
                out_ref[c, i, :, lanes] = value

            cell_update(load, first + i, write)
            return carry

        lax.fori_loop(0, HALO, step, 0)


def boundary_update(base_flow, adjoint, tails, heads, far_tails, far_heads, previous):
    comps, cells, span, rows = base_flow.shape
    full_spec = pl.BlockSpec((comps, cells, span, rows), lambda s: (0, 0, 0, 0))
    halo_spec = pl.BlockSpec((2, comps, HALO, span, rows), lambda s: (0, 0, 0, 0, 0))
    out_spec = pl.BlockSpec((comps, HALO, span, rows), lambda s: (0, s * (cells // HALO - 1), 0, 0))
    return pl.pallas_call(
        boundary_kernel,
        grid=(2,),
        in_specs=[full_spec, full_spec, halo_spec, halo_spec, halo_spec, halo_spec, pl.BlockSpec(memory_space=pl.ANY)],
        out_specs=out_spec,
        out_shape=jax.ShapeDtypeStruct(base_flow.shape, jnp.float32),
        scratch_shapes=[pltpu.VMEM((2, comps, cells + 2 * HALO, span, rows), jnp.float32)],
        input_output_aliases={6: 0},
    )(base_flow, adjoint, tails, heads, far_tails, far_heads, previous)


def body(base_flow, adjoint, first_op, second_op, far=()):
    comps, cells, spanwise, local_rows = base_flow.shape
    groups = lax.axis_size("gy")
    total_rows = local_rows * groups
    part = spanwise // groups

    base_low = lax.optimization_barrier(base_flow.astype(jnp.bfloat16))
    adjoint_low = lax.optimization_barrier(adjoint.astype(jnp.bfloat16))
    low = jnp.concatenate((base_low, adjoint_low), 0).reshape(2 * comps, cells, spanwise, 1, local_rows)
    lines = lax.all_to_all(low, "gy", split_axis=2, concat_axis=3, tiled=True)
    tail_cells = jnp.stack((base_flow[:, cells - HALO :], adjoint[:, cells - HALO :]), 0)
    head_cells = jnp.stack((base_flow[:, :HALO], adjoint[:, :HALO]), 0)
    tails = ring_shift(tail_cells, "gx", True, far, False)
    heads = ring_shift(head_cells, "gx", False, far, False)
    partial = interior_update(base_flow, adjoint)
    lines, partial, tails, heads, tail_cells, head_cells = lax.optimization_barrier(
        (lines, partial, tails, heads, tail_cells, head_cells)
    )
    far_tails = ring_shift(tail_cells, "gx", True, far, True)
    far_heads = ring_shift(head_cells, "gx", False, far, True)
    lines = lines.reshape(2 * comps, cells, part, total_rows)
    base_lines = lines[:comps]
    adj_lines = lines[comps:]
    slope_base = jnp.einsum("fxzk,ik->fxzi", base_lines, first_op, preferred_element_type=jnp.float32)
    slope_adj = jnp.einsum("fxzk,ik->fxzi", adj_lines, first_op, preferred_element_type=jnp.float32)
    curves = jnp.einsum("fxzk,ik->fxzi", adj_lines, second_op, preferred_element_type=jnp.float32)
    normal_vel = base_lines[1].astype(jnp.float32)
    coupling = jnp.sum(adj_lines.astype(jnp.float32) * slope_base, axis=0)
    wall_part = normal_vel[None] * slope_adj + VISCOSITY * curves
    wall_part = wall_part.at[1].add(-coupling)
    wall_part = wall_part.astype(jnp.bfloat16).reshape(comps, cells, part, groups, local_rows)
    wall_part, partial = lax.optimization_barrier((wall_part, partial))
    wall_part = lax.all_to_all(wall_part, "gy", split_axis=3, concat_axis=2, tiled=True)
    wall_part = wall_part.reshape(comps, cells, spanwise, local_rows).astype(jnp.float32)

    partial = boundary_update(base_flow, adjoint, tails, heads, far_tails, far_heads, partial)
    updated = partial + STEP_WEIGHT * wall_part
    wall_index = lax.axis_index("gy") * local_rows + jnp.arange(local_rows, dtype=jnp.int32)
    interior = (wall_index > 0) & (wall_index < total_rows - 1)
    return jnp.where(interior, updated, jnp.float32(0.0))


def far_links(mesh):
    devices = mesh.devices
    count = devices.shape[0]
    return tuple(
        bool(devices[i, 0].coords[1] != devices[(i + 1) % count, 0].coords[1]) for i in range(count)
    )


def solution(mesh):
    return jax.shard_map(
        functools.partial(body, far=far_links(mesh)),
        mesh=mesh,
        in_specs=(P(None, "gx", None, "gy"), P(None, "gx", None, "gy"), P(), P()),
        out_specs=P(None, "gx", None, "gy"),
        check_vma=False,
    )
```

```python
import functools

import jax
import jax.numpy as jnp
from jax import lax
from jax.experimental import pallas as pl
from jax.experimental.pallas import tpu as pltpu
from jax.sharding import PartitionSpec as P

C_FIRST = (0.8, -0.2, 4.0 / 105.0, -1.0 / 280.0)
C_SECOND = (1.6, -0.2, 8.0 / 315.0, -1.0 / 560.0)
C_CENTER = -205.0 / 72.0
VISCOSITY = 0.1
STEP_WEIGHT = 0.5
HALO = 4
LANES = 128


def ring_shift(value, axis, forward, far, want_far):
    count = lax.axis_size(axis)
    links = [i for i in range(count) if far[i] == want_far]
    if forward:
        pairs = [(i, (i + 1) % count) for i in links]
    else:
        pairs = [((i + 1) % count, i) for i in links]
    return lax.ppermute(value, axis, pairs)


def cell_update(load, x, write):
    span = load(0, 0, x).shape[0]

    def zshift(v, k):
        return pltpu.roll(v, (span - k) % span, 0)

    def derivs(field, c, second):
        center = load(field, c, x)
        plus = [load(field, c, x + k) for k in range(1, 5)]
        minus = [load(field, c, x - k) for k in range(1, 5)]
        zp = [zshift(center, k) for k in range(1, 5)]
        zm = [zshift(center, span - k) for k in range(1, 5)]
        dx = C_FIRST[0] * (plus[0] - minus[0])
        dz = C_FIRST[0] * (zp[0] - zm[0])
        for k in range(1, 4):
            dx = dx + C_FIRST[k] * (plus[k] - minus[k])
            dz = dz + C_FIRST[k] * (zp[k] - zm[k])
        if not second:
            return center, dx, dz, None, None
        dxx = C_CENTER * center
        dzz = C_CENTER * center
        for k in range(4):
            dxx = dxx + C_SECOND[k] * (plus[k] + minus[k])
            dzz = dzz + C_SECOND[k] * (zp[k] + zm[k])
        return center, dx, dz, dxx, dzz

    base = [derivs(0, j, False) for j in range(3)]
    adj = [derivs(1, c, True) for c in range(3)]
    first_coupling = adj[0][0] * base[0][1] + adj[1][0] * base[1][1] + adj[2][0] * base[2][1]
    last_coupling = adj[0][0] * base[0][2] + adj[1][0] * base[1][2] + adj[2][0] * base[2][2]
    for c in range(3):
        center, dx, dz, dxx, dzz = adj[c]
        tendency = base[0][0] * dx + base[2][0] * dz + VISCOSITY * (dxx + dzz)
        if c == 0:
            tendency = tendency - first_coupling
        elif c == 2:
            tendency = tendency - last_coupling
        write(c, center + STEP_WEIGHT * tendency)


def interior_kernel(base_ref, adj_ref, out_ref):
    first = (pl.program_id(1) + 1) * HALO

    def load(field, c, x):
        return (base_ref if field == 0 else adj_ref)[c, x]

    def step(i, carry):
        def write(c, value):
            out_ref[c, i] = value

        cell_update(load, first + i, write)
        return carry

    lax.fori_loop(0, HALO, step, 0)


def interior_update(base_flow, adjoint):
    comps, cells, span, rows = base_flow.shape
    field_spec = pl.BlockSpec((comps, cells, span, LANES), lambda j, b: (0, 0, 0, j))
    out_spec = pl.BlockSpec((comps, HALO, span, LANES), lambda j, b: (0, b + 1, 0, j))
    return pl.pallas_call(
        interior_kernel,
        grid=(rows // LANES, cells // HALO - 2),
        in_specs=[field_spec, field_spec],
        out_specs=out_spec,
        out_shape=jax.ShapeDtypeStruct(base_flow.shape, jnp.float32),
    )(base_flow, adjoint)


def boundary_kernel(base_ref, adj_ref, tail_ref, head_ref, far_tail_ref, far_head_ref, prev_ref, out_ref, ext_ref):
    comps, cells, span, rows = base_ref.shape
    side = pl.program_id(0)

    @pl.when(side == 0)
    def _():
        ext_ref[0, :, HALO : HALO + cells] = base_ref[...]
        ext_ref[1, :, HALO : HALO + cells] = adj_ref[...]
        ext_ref[:, :, :HALO] = tail_ref[...] + far_tail_ref[...]
        ext_ref[:, :, HALO + cells :] = head_ref[...] + far_head_ref[...]

    first = side * (cells - HALO)
    for lane in range(rows // LANES):
        lanes = pl.ds(lane * LANES, LANES)

        def load(field, c, x, lanes=lanes):
            return ext_ref[field, c, x + HALO, :, lanes]

        def step(i, carry, lanes=lanes, load=load):
            def write(c, value):
                out_ref[c, i, :, lanes] = value

            cell_update(load, first + i, write)
            return carry

        lax.fori_loop(0, HALO, step, 0)


def boundary_update(base_flow, adjoint, tails, heads, far_tails, far_heads, previous):
    comps, cells, span, rows = base_flow.shape
    full_spec = pl.BlockSpec((comps, cells, span, rows), lambda s: (0, 0, 0, 0))
    halo_spec = pl.BlockSpec((2, comps, HALO, span, rows), lambda s: (0, 0, 0, 0, 0))
    out_spec = pl.BlockSpec((comps, HALO, span, rows), lambda s: (0, s * (cells // HALO - 1), 0, 0))
    return pl.pallas_call(
        boundary_kernel,
        grid=(2,),
        in_specs=[full_spec, full_spec, halo_spec, halo_spec, halo_spec, halo_spec, pl.BlockSpec(memory_space=pl.ANY)],
        out_specs=out_spec,
        out_shape=jax.ShapeDtypeStruct(base_flow.shape, jnp.float32),
        scratch_shapes=[pltpu.VMEM((2, comps, cells + 2 * HALO, span, rows), jnp.float32)],
        input_output_aliases={6: 0},
    )(base_flow, adjoint, tails, heads, far_tails, far_heads, previous)


def body(base_flow, adjoint, first_op, second_op, far=()):
    comps, cells, spanwise, local_rows = base_flow.shape
    groups = lax.axis_size("gy")
    total_rows = local_rows * groups
    part = spanwise // groups

    base_low = lax.optimization_barrier(base_flow.astype(jnp.bfloat16))
    adjoint_low = lax.optimization_barrier(adjoint.astype(jnp.bfloat16))
    low = jnp.concatenate((base_low, adjoint_low), 0).reshape(2 * comps, cells, spanwise, 1, local_rows)
    lines = lax.all_to_all(low, "gy", split_axis=2, concat_axis=3, tiled=True)
    tail_cells = jnp.stack((base_flow[:, cells - HALO :], adjoint[:, cells - HALO :]), 0)
    head_cells = jnp.stack((base_flow[:, :HALO], adjoint[:, :HALO]), 0)
    tails = ring_shift(tail_cells, "gx", True, far, False)
    heads = ring_shift(head_cells, "gx", False, far, False)
    partial = interior_update(base_flow, adjoint)
    lines, partial, tails, heads, tail_cells, head_cells = lax.optimization_barrier(
        (lines, partial, tails, heads, tail_cells, head_cells)
    )
    far_tails, far_heads = far_exchange(tail_cells, head_cells, far)
    lines = lines.reshape(2 * comps, cells, part, total_rows)
    base_lines = lines[:comps]
    adj_lines = lines[comps:]
    slope_base = jnp.einsum("fxzk,ik->fxzi", base_lines, first_op, preferred_element_type=jnp.float32)
    slope_adj = jnp.einsum("fxzk,ik->fxzi", adj_lines, first_op, preferred_element_type=jnp.float32)
    curves = jnp.einsum("fxzk,ik->fxzi", adj_lines, second_op, preferred_element_type=jnp.float32)
    normal_vel = base_lines[1].astype(jnp.float32)
    coupling = jnp.sum(adj_lines.astype(jnp.float32) * slope_base, axis=0)
    wall_part = normal_vel[None] * slope_adj + VISCOSITY * curves
    wall_part = wall_part.at[1].add(-coupling)
    wall_part = wall_part.astype(jnp.bfloat16).reshape(comps, cells, part, groups, local_rows)
    wall_part, partial = lax.optimization_barrier((wall_part, partial))
    wall_part = lax.all_to_all(wall_part, "gy", split_axis=3, concat_axis=2, tiled=True)
    wall_part = wall_part.reshape(comps, cells, spanwise, local_rows).astype(jnp.float32)

    partial = boundary_update(base_flow, adjoint, tails, heads, far_tails, far_heads, partial)
    updated = partial + STEP_WEIGHT * wall_part
    wall_index = lax.axis_index("gy") * local_rows + jnp.arange(local_rows, dtype=jnp.int32)
    interior = (wall_index > 0) & (wall_index < total_rows - 1)
    return jnp.where(interior, updated, jnp.float32(0.0))


def far_exchange(tail_cells, head_cells, far):
    count = lax.axis_size("gx")
    links = [i for i in range(count) if far[i]]
    tail_senders = set(links)
    head_senders = {(i + 1) % count for i in links}
    if not links:
        return jnp.zeros_like(tail_cells), jnp.zeros_like(head_cells)
    if tail_senders & head_senders:
        return (
            ring_shift(tail_cells, "gx", True, far, True),
            ring_shift(head_cells, "gx", False, far, True),
        )
    pairs = [(i, (i + 1) % count) for i in links] + [((i + 1) % count, i) for i in links]
    position = lax.axis_index("gx")
    sends_tail = jnp.zeros((), jnp.bool_)
    for i in links:
        sends_tail = sends_tail | (position == i)
    received = lax.ppermute(jnp.where(sends_tail, tail_cells, head_cells), "gx", pairs)
    zero = jnp.zeros_like(received)
    gets_tail = jnp.zeros((), jnp.bool_)
    for i in links:
        gets_tail = gets_tail | (position == (i + 1) % count)
    return jnp.where(gets_tail, received, zero), jnp.where(sends_tail, received, zero)


def far_links(mesh):
    devices = mesh.devices
    count = devices.shape[0]
    return tuple(
        bool(devices[i, 0].coords[1] != devices[(i + 1) % count, 0].coords[1]) for i in range(count)
    )


def solution(mesh):
    return jax.shard_map(
        functools.partial(body, far=far_links(mesh)),
        mesh=mesh,
        in_specs=(P(None, "gx", None, "gy"), P(None, "gx", None, "gy"), P(), P()),
        out_specs=P(None, "gx", None, "gy"),
        check_vma=False,
    )
```

```python
import functools

import jax
import jax.numpy as jnp
from jax import lax
from jax.experimental import pallas as pl
from jax.experimental.pallas import tpu as pltpu
from jax.sharding import PartitionSpec as P

C_FIRST = (0.8, -0.2, 4.0 / 105.0, -1.0 / 280.0)
C_SECOND = (1.6, -0.2, 8.0 / 315.0, -1.0 / 560.0)
C_CENTER = -205.0 / 72.0
VISCOSITY = 0.1
STEP_WEIGHT = 0.5
HALO = 4
LANES = 128


def ring_shift(value, axis, forward, far, want_far):
    count = lax.axis_size(axis)
    links = [i for i in range(count) if far[i] == want_far]
    if forward:
        pairs = [(i, (i + 1) % count) for i in links]
    else:
        pairs = [((i + 1) % count, i) for i in links]
    return lax.ppermute(value, axis, pairs)


def cell_update(load, x, write):
    span = load(0, 0, x).shape[0]

    def zshift(v, k):
        return pltpu.roll(v, (span - k) % span, 0)

    def derivs(field, c, second):
        center = load(field, c, x)
        plus = [load(field, c, x + k) for k in range(1, 5)]
        minus = [load(field, c, x - k) for k in range(1, 5)]
        zp = [zshift(center, k) for k in range(1, 5)]
        zm = [zshift(center, span - k) for k in range(1, 5)]
        dx = C_FIRST[0] * (plus[0] - minus[0])
        dz = C_FIRST[0] * (zp[0] - zm[0])
        for k in range(1, 4):
            dx = dx + C_FIRST[k] * (plus[k] - minus[k])
            dz = dz + C_FIRST[k] * (zp[k] - zm[k])
        if not second:
            return center, dx, dz, None, None
        dxx = C_CENTER * center
        dzz = C_CENTER * center
        for k in range(4):
            dxx = dxx + C_SECOND[k] * (plus[k] + minus[k])
            dzz = dzz + C_SECOND[k] * (zp[k] + zm[k])
        return center, dx, dz, dxx, dzz

    base = [derivs(0, j, False) for j in range(3)]
    adj = [derivs(1, c, True) for c in range(3)]
    first_coupling = adj[0][0] * base[0][1] + adj[1][0] * base[1][1] + adj[2][0] * base[2][1]
    last_coupling = adj[0][0] * base[0][2] + adj[1][0] * base[1][2] + adj[2][0] * base[2][2]
    for c in range(3):
        center, dx, dz, dxx, dzz = adj[c]
        tendency = base[0][0] * dx + base[2][0] * dz + VISCOSITY * (dxx + dzz)
        if c == 0:
            tendency = tendency - first_coupling
        elif c == 2:
            tendency = tendency - last_coupling
        write(c, center + STEP_WEIGHT * tendency)


def interior_kernel(base_ref, adj_ref, out_ref):
    first = (pl.program_id(1) + 1) * HALO

    def load(field, c, x):
        return (base_ref if field == 0 else adj_ref)[c, x]

    def step(i, carry):
        def write(c, value):
            out_ref[c, i] = value

        cell_update(load, first + i, write)
        return carry

    lax.fori_loop(0, HALO, step, 0)


def interior_update(base_flow, adjoint):
    comps, cells, span, rows = base_flow.shape
    field_spec = pl.BlockSpec((comps, cells, span, LANES), lambda j, b: (0, 0, 0, j))
    out_spec = pl.BlockSpec((comps, HALO, span, LANES), lambda j, b: (0, b + 1, 0, j))
    return pl.pallas_call(
        interior_kernel,
        grid=(rows // LANES, cells // HALO - 2),
        in_specs=[field_spec, field_spec],
        out_specs=out_spec,
        out_shape=jax.ShapeDtypeStruct(base_flow.shape, jnp.float32),
    )(base_flow, adjoint)


def boundary_kernel(flag_ref, base_ref, adj_ref, tail_ref, head_ref, far_ref, prev_ref, out_ref, ext_ref):
    comps, cells, span, rows = base_ref.shape
    side = pl.program_id(0)

    @pl.when(side == 0)
    def _():
        ext_ref[0, :, HALO : HALO + cells] = base_ref[...]
        ext_ref[1, :, HALO : HALO + cells] = adj_ref[...]
        ext_ref[:, :, :HALO] = tail_ref[...]
        ext_ref[:, :, HALO + cells :] = head_ref[...]

        @pl.when(flag_ref[0] == 1)
        def _():
            ext_ref[:, :, :HALO] = far_ref[...]

        @pl.when(flag_ref[1] == 1)
        def _():
            ext_ref[:, :, HALO + cells :] = far_ref[...]

    first = side * (cells - HALO)
    for lane in range(rows // LANES):
        lanes = pl.ds(lane * LANES, LANES)

        def load(field, c, x, lanes=lanes):
            return ext_ref[field, c, x + HALO, :, lanes]

        def step(i, carry, lanes=lanes, load=load):
            def write(c, value):
                out_ref[c, i, :, lanes] = value

            cell_update(load, first + i, write)
            return carry

        lax.fori_loop(0, HALO, step, 0)


def boundary_update(base_flow, adjoint, tails, heads, far_cells, far_flags, previous):
    comps, cells, span, rows = base_flow.shape
    full_spec = pl.BlockSpec((comps, cells, span, rows), lambda s: (0, 0, 0, 0))
    halo_spec = pl.BlockSpec((2, comps, HALO, span, rows), lambda s: (0, 0, 0, 0, 0))
    out_spec = pl.BlockSpec((comps, HALO, span, rows), lambda s: (0, s * (cells // HALO - 1), 0, 0))
    return pl.pallas_call(
        boundary_kernel,
        grid=(2,),
        in_specs=[
            pl.BlockSpec(memory_space=pltpu.SMEM),
            full_spec,
            full_spec,
            halo_spec,
            halo_spec,
            halo_spec,
            pl.BlockSpec(memory_space=pl.ANY),
        ],
        out_specs=out_spec,
        out_shape=jax.ShapeDtypeStruct(base_flow.shape, jnp.float32),
        scratch_shapes=[pltpu.VMEM((2, comps, cells + 2 * HALO, span, rows), jnp.float32)],
        input_output_aliases={6: 0},
    )(far_flags, base_flow, adjoint, tails, heads, far_cells, previous)


def body(base_flow, adjoint, first_op, second_op, far=()):
    comps, cells, spanwise, local_rows = base_flow.shape
    groups = lax.axis_size("gy")
    total_rows = local_rows * groups
    part = spanwise // groups

    base_low = lax.optimization_barrier(base_flow.astype(jnp.bfloat16))
    adjoint_low = lax.optimization_barrier(adjoint.astype(jnp.bfloat16))
    low = jnp.concatenate((base_low, adjoint_low), 0).reshape(2 * comps, cells, spanwise, 1, local_rows)
    lines = lax.all_to_all(low, "gy", split_axis=2, concat_axis=3, tiled=True)
    tail_cells = jnp.stack((base_flow[:, cells - HALO :], adjoint[:, cells - HALO :]), 0)
    head_cells = jnp.stack((base_flow[:, :HALO], adjoint[:, :HALO]), 0)
    tails = ring_shift(tail_cells, "gx", True, far, False)
    heads = ring_shift(head_cells, "gx", False, far, False)
    partial = interior_update(base_flow, adjoint)
    lines, partial, tails, heads, tail_cells, head_cells = lax.optimization_barrier(
        (lines, partial, tails, heads, tail_cells, head_cells)
    )
    far_cells, far_flags = far_exchange(tail_cells, head_cells, far)
    lines = lines.reshape(2 * comps, cells, part, total_rows)
    base_lines = lines[:comps]
    adj_lines = lines[comps:]
    slope_base = jnp.einsum("fxzk,ik->fxzi", base_lines, first_op, preferred_element_type=jnp.float32)
    slope_adj = jnp.einsum("fxzk,ik->fxzi", adj_lines, first_op, preferred_element_type=jnp.float32)
    curves = jnp.einsum("fxzk,ik->fxzi", adj_lines, second_op, preferred_element_type=jnp.float32)
    normal_vel = base_lines[1].astype(jnp.float32)
    coupling = jnp.sum(adj_lines.astype(jnp.float32) * slope_base, axis=0)
    wall_part = normal_vel[None] * slope_adj + VISCOSITY * curves
    wall_part = wall_part.at[1].add(-coupling)
    wall_part = wall_part.astype(jnp.bfloat16).reshape(comps, cells, part, groups, local_rows)
    wall_part, partial = lax.optimization_barrier((wall_part, partial))
    wall_part = lax.all_to_all(wall_part, "gy", split_axis=3, concat_axis=2, tiled=True)
    wall_part = wall_part.reshape(comps, cells, spanwise, local_rows).astype(jnp.float32)

    partial = boundary_update(base_flow, adjoint, tails, heads, far_cells, far_flags, partial)
    updated = partial + STEP_WEIGHT * wall_part
    wall_index = lax.axis_index("gy") * local_rows + jnp.arange(local_rows, dtype=jnp.int32)
    interior = (wall_index > 0) & (wall_index < total_rows - 1)
    return jnp.where(interior, updated, jnp.float32(0.0))


def far_exchange(tail_cells, head_cells, far):
    count = lax.axis_size("gx")
    links = [i for i in range(count) if far[i]]
    tail_senders = {i for i in links}
    head_senders = {(i + 1) % count for i in links}
    assert links and not (tail_senders & head_senders)
    pairs = [(i, (i + 1) % count) for i in links] + [((i + 1) % count, i) for i in links]
    position = lax.axis_index("gx")
    sends_tail = jnp.zeros((), jnp.bool_)
    gets_tail = jnp.zeros((), jnp.bool_)
    for i in links:
        sends_tail = sends_tail | (position == i)
        gets_tail = gets_tail | (position == (i + 1) % count)
    received = lax.ppermute(jnp.where(sends_tail, tail_cells, head_cells), "gx", pairs)
    flags = jnp.stack((gets_tail, sends_tail)).astype(jnp.int32)
    return received, flags


def far_links(mesh):
    devices = mesh.devices
    count = devices.shape[0]
    return tuple(
        bool(devices[i, 0].coords[1] != devices[(i + 1) % count, 0].coords[1]) for i in range(count)
    )


def solution(mesh):
    return jax.shard_map(
        functools.partial(body, far=far_links(mesh)),
        mesh=mesh,
        in_specs=(P(None, "gx", None, "gy"), P(None, "gx", None, "gy"), P(), P()),
        out_specs=P(None, "gx", None, "gy"),
        check_vma=False,
    )
```

```python
import functools

import jax
import jax.numpy as jnp
from jax import lax
from jax.experimental import pallas as pl
from jax.experimental.pallas import tpu as pltpu
from jax.sharding import PartitionSpec as P

C_FIRST = (0.8, -0.2, 4.0 / 105.0, -1.0 / 280.0)
C_SECOND = (1.6, -0.2, 8.0 / 315.0, -1.0 / 560.0)
C_CENTER = -205.0 / 72.0
VISCOSITY = 0.1
STEP_WEIGHT = 0.5
HALO = 4
LANES = 128


def ring_shift(value, axis, forward, far, want_far):
    count = lax.axis_size(axis)
    links = [i for i in range(count) if far[i] == want_far]
    if forward:
        pairs = [(i, (i + 1) % count) for i in links]
    else:
        pairs = [((i + 1) % count, i) for i in links]
    return lax.ppermute(value, axis, pairs)


def cell_update(load, x, write):
    span = load(0, 0, x).shape[0]

    def zshift(v, k):
        return pltpu.roll(v, (span - k) % span, 0)

    def derivs(field, c, second):
        center = load(field, c, x)
        plus = [load(field, c, x + k) for k in range(1, 5)]
        minus = [load(field, c, x - k) for k in range(1, 5)]
        zp = [zshift(center, k) for k in range(1, 5)]
        zm = [zshift(center, span - k) for k in range(1, 5)]
        dx = C_FIRST[0] * (plus[0] - minus[0])
        dz = C_FIRST[0] * (zp[0] - zm[0])
        for k in range(1, 4):
            dx = dx + C_FIRST[k] * (plus[k] - minus[k])
            dz = dz + C_FIRST[k] * (zp[k] - zm[k])
        if not second:
            return center, dx, dz, None, None
        dxx = C_CENTER * center
        dzz = C_CENTER * center
        for k in range(4):
            dxx = dxx + C_SECOND[k] * (plus[k] + minus[k])
            dzz = dzz + C_SECOND[k] * (zp[k] + zm[k])
        return center, dx, dz, dxx, dzz

    base = [derivs(0, j, False) for j in range(3)]
    adj = [derivs(1, c, True) for c in range(3)]
    first_coupling = adj[0][0] * base[0][1] + adj[1][0] * base[1][1] + adj[2][0] * base[2][1]
    last_coupling = adj[0][0] * base[0][2] + adj[1][0] * base[1][2] + adj[2][0] * base[2][2]
    for c in range(3):
        center, dx, dz, dxx, dzz = adj[c]
        tendency = base[0][0] * dx + base[2][0] * dz + VISCOSITY * (dxx + dzz)
        if c == 0:
            tendency = tendency - first_coupling
        elif c == 2:
            tendency = tendency - last_coupling
        write(c, center + STEP_WEIGHT * tendency)


def interior_kernel(base_ref, adj_ref, out_ref):
    first = (pl.program_id(1) + 1) * HALO

    def load(field, c, x):
        return (base_ref if field == 0 else adj_ref)[c, x]

    def step(i, carry):
        def write(c, value):
            out_ref[c, i] = value

        cell_update(load, first + i, write)
        return carry

    lax.fori_loop(0, HALO, step, 0)


def interior_update(base_flow, adjoint):
    comps, cells, span, rows = base_flow.shape
    field_spec = pl.BlockSpec((comps, cells, span, LANES), lambda j, b: (0, 0, 0, j))
    out_spec = pl.BlockSpec((comps, HALO, span, LANES), lambda j, b: (0, b + 1, 0, j))
    return pl.pallas_call(
        interior_kernel,
        grid=(rows // LANES, cells // HALO - 2),
        in_specs=[field_spec, field_spec],
        out_specs=out_spec,
        out_shape=jax.ShapeDtypeStruct(base_flow.shape, jnp.float32),
    )(base_flow, adjoint)


def boundary_kernel(base_ref, adj_ref, tail_ref, head_ref, far_tail_ref, far_head_ref, prev_ref, out_ref, ext_ref):
    comps, cells, span, rows = base_ref.shape
    side = pl.program_id(0)

    @pl.when(side == 0)
    def _():
        ext_ref[0, :, HALO : HALO + cells] = base_ref[...]
        ext_ref[1, :, HALO : HALO + cells] = adj_ref[...]
        ext_ref[:, :, :HALO] = tail_ref[...] + far_tail_ref[...]
        ext_ref[:, :, HALO + cells :] = head_ref[...] + far_head_ref[...]

    first = side * (cells - HALO)
    for lane in range(rows // LANES):
        lanes = pl.ds(lane * LANES, LANES)

        def load(field, c, x, lanes=lanes):
            return ext_ref[field, c, x + HALO, :, lanes]

        def step(i, carry, lanes=lanes, load=load):
            def write(c, value):
                out_ref[c, i, :, lanes] = value

            cell_update(load, first + i, write)
            return carry

        lax.fori_loop(0, HALO, step, 0)


def boundary_update(base_flow, adjoint, tails, heads, far_tails, far_heads, previous):
    comps, cells, span, rows = base_flow.shape
    full_spec = pl.BlockSpec((comps, cells, span, rows), lambda s: (0, 0, 0, 0))
    halo_spec = pl.BlockSpec((2, comps, HALO, span, rows), lambda s: (0, 0, 0, 0, 0))
    out_spec = pl.BlockSpec((comps, HALO, span, rows), lambda s: (0, s * (cells // HALO - 1), 0, 0))
    return pl.pallas_call(
        boundary_kernel,
        grid=(2,),
        in_specs=[full_spec, full_spec, halo_spec, halo_spec, halo_spec, halo_spec, pl.BlockSpec(memory_space=pl.ANY)],
        out_specs=out_spec,
        out_shape=jax.ShapeDtypeStruct(base_flow.shape, jnp.float32),
        scratch_shapes=[pltpu.VMEM((2, comps, cells + 2 * HALO, span, rows), jnp.float32)],
        input_output_aliases={6: 0},
    )(base_flow, adjoint, tails, heads, far_tails, far_heads, previous)


def body(base_flow, adjoint, first_op, second_op, far=()):
    comps, cells, spanwise, local_rows = base_flow.shape
    groups = lax.axis_size("gy")
    total_rows = local_rows * groups
    part = spanwise // groups

    base_low = lax.optimization_barrier(base_flow.astype(jnp.bfloat16))
    adjoint_low = lax.optimization_barrier(adjoint.astype(jnp.bfloat16))
    low = jnp.concatenate((base_low, adjoint_low), 0).reshape(2 * comps, cells, spanwise, 1, local_rows)
    lines = lax.all_to_all(low, "gy", split_axis=2, concat_axis=3, tiled=True)
    tail_cells = jnp.stack((base_flow[:, cells - HALO :], adjoint[:, cells - HALO :]), 0)
    head_cells = jnp.stack((base_flow[:, :HALO], adjoint[:, :HALO]), 0)
    tails = ring_shift(tail_cells, "gx", True, far, False)
    heads = ring_shift(head_cells, "gx", False, far, False)
    far_pairs, sends_tail, gets_tail = far_plan(far)
    far_send = jnp.where(sends_tail, tail_cells, head_cells)
    partial = interior_update(base_flow, adjoint)
    lines, partial, tails, heads, far_send = lax.optimization_barrier((lines, partial, tails, heads, far_send))
    received = lax.ppermute(far_send, "gx", far_pairs)
    zero = jnp.zeros_like(received)
    far_tails = jnp.where(gets_tail, received, zero)
    far_heads = jnp.where(sends_tail, received, zero)
    lines = lines.reshape(2 * comps, cells, part, total_rows)
    base_lines = lines[:comps]
    adj_lines = lines[comps:]
    slope_base = jnp.einsum("fxzk,ik->fxzi", base_lines, first_op, preferred_element_type=jnp.float32)
    slope_adj = jnp.einsum("fxzk,ik->fxzi", adj_lines, first_op, preferred_element_type=jnp.float32)
    curves = jnp.einsum("fxzk,ik->fxzi", adj_lines, second_op, preferred_element_type=jnp.float32)
    normal_vel = base_lines[1].astype(jnp.float32)
    coupling = jnp.sum(adj_lines.astype(jnp.float32) * slope_base, axis=0)
    wall_part = normal_vel[None] * slope_adj + VISCOSITY * curves
    wall_part = wall_part.at[1].add(-coupling)
    wall_part = wall_part.astype(jnp.bfloat16).reshape(comps, cells, part, groups, local_rows)
    wall_part, partial = lax.optimization_barrier((wall_part, partial))
    wall_part = lax.all_to_all(wall_part, "gy", split_axis=3, concat_axis=2, tiled=True)
    wall_part = wall_part.reshape(comps, cells, spanwise, local_rows).astype(jnp.float32)

    partial = boundary_update(base_flow, adjoint, tails, heads, far_tails, far_heads, partial)
    updated = partial + STEP_WEIGHT * wall_part
    wall_index = lax.axis_index("gy") * local_rows + jnp.arange(local_rows, dtype=jnp.int32)
    interior = (wall_index > 0) & (wall_index < total_rows - 1)
    return jnp.where(interior, updated, jnp.float32(0.0))


def far_plan(far):
    count = lax.axis_size("gx")
    links = [i for i in range(count) if far[i]]
    tail_senders = {i for i in links}
    head_senders = {(i + 1) % count for i in links}
    assert links and not (tail_senders & head_senders)
    pairs = [(i, (i + 1) % count) for i in links] + [((i + 1) % count, i) for i in links]
    position = lax.axis_index("gx")
    sends_tail = jnp.zeros((), jnp.bool_)
    gets_tail = jnp.zeros((), jnp.bool_)
    for i in links:
        sends_tail = sends_tail | (position == i)
        gets_tail = gets_tail | (position == (i + 1) % count)
    return pairs, sends_tail, gets_tail


def far_links(mesh):
    devices = mesh.devices
    count = devices.shape[0]
    return tuple(
        bool(devices[i, 0].coords[1] != devices[(i + 1) % count, 0].coords[1]) for i in range(count)
    )


def solution(mesh):
    return jax.shard_map(
        functools.partial(body, far=far_links(mesh)),
        mesh=mesh,
        in_specs=(P(None, "gx", None, "gy"), P(None, "gx", None, "gy"), P(), P()),
        out_specs=P(None, "gx", None, "gy"),
        check_vma=False,
    )
```

```python
import functools

import jax
import jax.numpy as jnp
from jax import lax
from jax.experimental import pallas as pl
from jax.experimental.pallas import tpu as pltpu
from jax.sharding import PartitionSpec as P

C_FIRST = (0.8, -0.2, 4.0 / 105.0, -1.0 / 280.0)
C_SECOND = (1.6, -0.2, 8.0 / 315.0, -1.0 / 560.0)
C_CENTER = -205.0 / 72.0
VISCOSITY = 0.1
STEP_WEIGHT = 0.5
HALO = 4
LANES = 128


def ring_shift(value, axis, forward, far, want_far):
    count = lax.axis_size(axis)
    links = [i for i in range(count) if far[i] == want_far]
    if forward:
        pairs = [(i, (i + 1) % count) for i in links]
    else:
        pairs = [((i + 1) % count, i) for i in links]
    return lax.ppermute(value, axis, pairs)


def cell_update(load, x, write):
    span = load(0, 0, x).shape[0]

    def zshift(v, k):
        return pltpu.roll(v, (span - k) % span, 0)

    def derivs(field, c, second):
        center = load(field, c, x)
        plus = [load(field, c, x + k) for k in range(1, 5)]
        minus = [load(field, c, x - k) for k in range(1, 5)]
        zp = [zshift(center, k) for k in range(1, 5)]
        zm = [zshift(center, span - k) for k in range(1, 5)]
        dx = C_FIRST[0] * (plus[0] - minus[0])
        dz = C_FIRST[0] * (zp[0] - zm[0])
        for k in range(1, 4):
            dx = dx + C_FIRST[k] * (plus[k] - minus[k])
            dz = dz + C_FIRST[k] * (zp[k] - zm[k])
        if not second:
            return center, dx, dz, None, None
        dxx = C_CENTER * center
        dzz = C_CENTER * center
        for k in range(4):
            dxx = dxx + C_SECOND[k] * (plus[k] + minus[k])
            dzz = dzz + C_SECOND[k] * (zp[k] + zm[k])
        return center, dx, dz, dxx, dzz

    base = [derivs(0, j, False) for j in range(3)]
    adj = [derivs(1, c, True) for c in range(3)]
    first_coupling = adj[0][0] * base[0][1] + adj[1][0] * base[1][1] + adj[2][0] * base[2][1]
    last_coupling = adj[0][0] * base[0][2] + adj[1][0] * base[1][2] + adj[2][0] * base[2][2]
    for c in range(3):
        center, dx, dz, dxx, dzz = adj[c]
        tendency = base[0][0] * dx + base[2][0] * dz + VISCOSITY * (dxx + dzz)
        if c == 0:
            tendency = tendency - first_coupling
        elif c == 2:
            tendency = tendency - last_coupling
        write(c, center + STEP_WEIGHT * tendency)


def interior_kernel(base_ref, adj_ref, out_ref):
    first = (pl.program_id(1) + 1) * HALO

    def load(field, c, x):
        return (base_ref if field == 0 else adj_ref)[c, x]

    def step(i, carry):
        def write(c, value):
            out_ref[c, i] = value

        cell_update(load, first + i, write)
        return carry

    lax.fori_loop(0, HALO, step, 0)


def interior_update(base_flow, adjoint):
    comps, cells, span, rows = base_flow.shape
    field_spec = pl.BlockSpec((comps, cells, span, LANES), lambda j, b: (0, 0, 0, j))
    out_spec = pl.BlockSpec((comps, HALO, span, LANES), lambda j, b: (0, b + 1, 0, j))
    return pl.pallas_call(
        interior_kernel,
        grid=(rows // LANES, cells // HALO - 2),
        in_specs=[field_spec, field_spec],
        out_specs=out_spec,
        out_shape=jax.ShapeDtypeStruct(base_flow.shape, jnp.float32),
    )(base_flow, adjoint)


def boundary_kernel(base_ref, adj_ref, tail_ref, head_ref, prev_ref, out_ref, ext_ref):
    comps, cells, span, rows = base_ref.shape
    side = pl.program_id(0)

    @pl.when(side == 0)
    def _():
        ext_ref[0, :, HALO : HALO + cells] = base_ref[...]
        ext_ref[1, :, HALO : HALO + cells] = adj_ref[...]
        ext_ref[:, :, :HALO] = tail_ref[...]
        ext_ref[:, :, HALO + cells :] = head_ref[...]

    first = side * (cells - HALO)
    for lane in range(rows // LANES):
        lanes = pl.ds(lane * LANES, LANES)

        def load(field, c, x, lanes=lanes):
            return ext_ref[field, c, x + HALO, :, lanes]

        def step(i, carry, lanes=lanes, load=load):
            def write(c, value):
                out_ref[c, i, :, lanes] = value

            cell_update(load, first + i, write)
            return carry

        lax.fori_loop(0, HALO, step, 0)


def boundary_update(base_flow, adjoint, tails, heads, previous):
    comps, cells, span, rows = base_flow.shape
    full_spec = pl.BlockSpec((comps, cells, span, rows), lambda s: (0, 0, 0, 0))
    halo_spec = pl.BlockSpec((2, comps, HALO, span, rows), lambda s: (0, 0, 0, 0, 0))
    out_spec = pl.BlockSpec((comps, HALO, span, rows), lambda s: (0, s * (cells // HALO - 1), 0, 0))
    return pl.pallas_call(
        boundary_kernel,
        grid=(2,),
        in_specs=[full_spec, full_spec, halo_spec, halo_spec, pl.BlockSpec(memory_space=pl.ANY)],
        out_specs=out_spec,
        out_shape=jax.ShapeDtypeStruct(base_flow.shape, jnp.float32),
        scratch_shapes=[pltpu.VMEM((2, comps, cells + 2 * HALO, span, rows), jnp.float32)],
        input_output_aliases={4: 0},
    )(base_flow, adjoint, tails, heads, previous)


def side_kernel(side_ref, base_ref, adj_ref, halo_ref, prev_ref, out_ref, ext_ref):
    comps, near, span, rows = base_ref.shape

    @pl.when(side_ref[0] == 0)
    def _():
        ext_ref[:, :, :HALO] = halo_ref[...]
        ext_ref[0, :, HALO:] = base_ref[...]
        ext_ref[1, :, HALO:] = adj_ref[...]

    @pl.when(side_ref[0] != 0)
    def _():
        ext_ref[0, :, :near] = base_ref[...]
        ext_ref[1, :, :near] = adj_ref[...]
        ext_ref[:, :, near:] = halo_ref[...]

    for lane in range(rows // LANES):
        lanes = pl.ds(lane * LANES, LANES)

        def load(field, c, x, lanes=lanes):
            return ext_ref[field, c, x, :, lanes]

        def step(i, carry, lanes=lanes, load=load):
            def write(c, value):
                out_ref[c, i, :, lanes] = value

            cell_update(load, HALO + i, write)
            return carry

        lax.fori_loop(0, HALO, step, 0)


def side_update(base_flow, adjoint, halo, side, previous):
    comps, cells, span, rows = base_flow.shape
    near = 2 * HALO
    last = cells // near - 1
    body_spec = pl.BlockSpec((comps, near, span, rows), lambda i, side_ref: (0, side_ref[0] * last, 0, 0))
    halo_spec = pl.BlockSpec((2, comps, HALO, span, rows), lambda i, side_ref: (0, 0, 0, 0, 0))
    out_spec = pl.BlockSpec(
        (comps, HALO, span, rows), lambda i, side_ref: (0, side_ref[0] * (cells // HALO - 1), 0, 0)
    )
    grid_spec = pltpu.PrefetchScalarGridSpec(
        num_scalar_prefetch=1,
        grid=(1,),
        in_specs=[body_spec, body_spec, halo_spec, pl.BlockSpec(memory_space=pl.ANY)],
        out_specs=out_spec,
        scratch_shapes=[pltpu.VMEM((2, comps, near + HALO, span, rows), jnp.float32)],
    )
    return pl.pallas_call(
        side_kernel,
        grid_spec=grid_spec,
        out_shape=jax.ShapeDtypeStruct(base_flow.shape, jnp.float32),
        input_output_aliases={4: 0},
    )(side, base_flow, adjoint, halo, previous)


def body(base_flow, adjoint, first_op, second_op, far=()):
    comps, cells, spanwise, local_rows = base_flow.shape
    groups = lax.axis_size("gy")
    total_rows = local_rows * groups
    part = spanwise // groups

    base_low = lax.optimization_barrier(base_flow.astype(jnp.bfloat16))
    adjoint_low = lax.optimization_barrier(adjoint.astype(jnp.bfloat16))
    low = jnp.concatenate((base_low, adjoint_low), 0).reshape(2 * comps, cells, spanwise, 1, local_rows)
    lines = lax.all_to_all(low, "gy", split_axis=2, concat_axis=3, tiled=True)
    tail_cells = jnp.stack((base_flow[:, cells - HALO :], adjoint[:, cells - HALO :]), 0)
    head_cells = jnp.stack((base_flow[:, :HALO], adjoint[:, :HALO]), 0)
    tails = ring_shift(tail_cells, "gx", True, far, False)
    heads = ring_shift(head_cells, "gx", False, far, False)
    far_pairs, sends_tail, gets_tail = far_plan(far)
    far_send = jnp.where(sends_tail, tail_cells, head_cells)
    partial = interior_update(base_flow, adjoint)
    lines, partial, tails, heads, far_send = lax.optimization_barrier((lines, partial, tails, heads, far_send))
    received = lax.ppermute(far_send, "gx", far_pairs)
    far_side = jnp.where(sends_tail, 1, 0).astype(jnp.int32).reshape(1)
    side_halo = jnp.where(gets_tail | sends_tail, received, tails)
    lines = lines.reshape(2 * comps, cells, part, total_rows)
    base_lines = lines[:comps]
    adj_lines = lines[comps:]
    slope_base = jnp.einsum("fxzk,ik->fxzi", base_lines, first_op, preferred_element_type=jnp.float32)
    slope_adj = jnp.einsum("fxzk,ik->fxzi", adj_lines, first_op, preferred_element_type=jnp.float32)
    curves = jnp.einsum("fxzk,ik->fxzi", adj_lines, second_op, preferred_element_type=jnp.float32)
    normal_vel = base_lines[1].astype(jnp.float32)
    coupling = jnp.sum(adj_lines.astype(jnp.float32) * slope_base, axis=0)
    wall_part = normal_vel[None] * slope_adj + VISCOSITY * curves
    wall_part = wall_part.at[1].add(-coupling)
    wall_part = wall_part.astype(jnp.bfloat16).reshape(comps, cells, part, groups, local_rows)
    wall_part, partial = lax.optimization_barrier((wall_part, partial))
    wall_part = lax.all_to_all(wall_part, "gy", split_axis=3, concat_axis=2, tiled=True)
    wall_part = wall_part.reshape(comps, cells, spanwise, local_rows).astype(jnp.float32)

    partial = boundary_update(base_flow, adjoint, tails, heads, partial)
    partial = side_update(base_flow, adjoint, side_halo, far_side, partial)
    updated = partial + STEP_WEIGHT * wall_part
    wall_index = lax.axis_index("gy") * local_rows + jnp.arange(local_rows, dtype=jnp.int32)
    interior = (wall_index > 0) & (wall_index < total_rows - 1)
    return jnp.where(interior, updated, jnp.float32(0.0))


def far_plan(far):
    count = lax.axis_size("gx")
    links = [i for i in range(count) if far[i]]
    tail_senders = {i for i in links}
    head_senders = {(i + 1) % count for i in links}
    assert links and not (tail_senders & head_senders)
    pairs = [(i, (i + 1) % count) for i in links] + [((i + 1) % count, i) for i in links]
    position = lax.axis_index("gx")
    sends_tail = jnp.zeros((), jnp.bool_)
    gets_tail = jnp.zeros((), jnp.bool_)
    for i in links:
        sends_tail = sends_tail | (position == i)
        gets_tail = gets_tail | (position == (i + 1) % count)
    return pairs, sends_tail, gets_tail


def far_links(mesh):
    devices = mesh.devices
    count = devices.shape[0]
    return tuple(
        bool(devices[i, 0].coords[1] != devices[(i + 1) % count, 0].coords[1]) for i in range(count)
    )


def solution(mesh):
    return jax.shard_map(
        functools.partial(body, far=far_links(mesh)),
        mesh=mesh,
        in_specs=(P(None, "gx", None, "gy"), P(None, "gx", None, "gy"), P(), P()),
        out_specs=P(None, "gx", None, "gy"),
        check_vma=False,
    )
```

```python
import functools

import jax
import jax.numpy as jnp
from jax import lax
from jax.experimental import pallas as pl
from jax.experimental.pallas import tpu as pltpu
from jax.sharding import PartitionSpec as P

C_FIRST = (0.8, -0.2, 4.0 / 105.0, -1.0 / 280.0)
C_SECOND = (1.6, -0.2, 8.0 / 315.0, -1.0 / 560.0)
C_CENTER = -205.0 / 72.0
VISCOSITY = 0.1
STEP_WEIGHT = 0.5
HALO = 4
LANES = 128


def ring_shift(value, axis, forward, far, want_far):
    count = lax.axis_size(axis)
    links = [i for i in range(count) if far[i] == want_far]
    if forward:
        pairs = [(i, (i + 1) % count) for i in links]
    else:
        pairs = [((i + 1) % count, i) for i in links]
    return lax.ppermute(value, axis, pairs)


def cell_update(load, x, write):
    span = load(0, 0, x).shape[0]

    def zshift(v, k):
        return pltpu.roll(v, (span - k) % span, 0)

    def derivs(field, c, second):
        center = load(field, c, x)
        plus = [load(field, c, x + k) for k in range(1, 5)]
        minus = [load(field, c, x - k) for k in range(1, 5)]
        zp = [zshift(center, k) for k in range(1, 5)]
        zm = [zshift(center, span - k) for k in range(1, 5)]
        dx = C_FIRST[0] * (plus[0] - minus[0])
        dz = C_FIRST[0] * (zp[0] - zm[0])
        for k in range(1, 4):
            dx = dx + C_FIRST[k] * (plus[k] - minus[k])
            dz = dz + C_FIRST[k] * (zp[k] - zm[k])
        if not second:
            return center, dx, dz, None, None
        dxx = C_CENTER * center
        dzz = C_CENTER * center
        for k in range(4):
            dxx = dxx + C_SECOND[k] * (plus[k] + minus[k])
            dzz = dzz + C_SECOND[k] * (zp[k] + zm[k])
        return center, dx, dz, dxx, dzz

    base = [derivs(0, j, False) for j in range(3)]
    adj = [derivs(1, c, True) for c in range(3)]
    first_coupling = adj[0][0] * base[0][1] + adj[1][0] * base[1][1] + adj[2][0] * base[2][1]
    last_coupling = adj[0][0] * base[0][2] + adj[1][0] * base[1][2] + adj[2][0] * base[2][2]
    for c in range(3):
        center, dx, dz, dxx, dzz = adj[c]
        tendency = base[0][0] * dx + base[2][0] * dz + VISCOSITY * (dxx + dzz)
        if c == 0:
            tendency = tendency - first_coupling
        elif c == 2:
            tendency = tendency - last_coupling
        write(c, center + STEP_WEIGHT * tendency)


def interior_kernel(base_ref, adj_ref, out_ref):
    first = (pl.program_id(1) + 1) * HALO

    def load(field, c, x):
        return (base_ref if field == 0 else adj_ref)[c, x]

    def step(i, carry):
        def write(c, value):
            out_ref[c, i] = value

        cell_update(load, first + i, write)
        return carry

    lax.fori_loop(0, HALO, step, 0)


def interior_update(base_flow, adjoint):
    comps, cells, span, rows = base_flow.shape
    field_spec = pl.BlockSpec((comps, cells, span, LANES), lambda j, b: (0, 0, 0, j))
    out_spec = pl.BlockSpec((comps, HALO, span, LANES), lambda j, b: (0, b + 1, 0, j))
    return pl.pallas_call(
        interior_kernel,
        grid=(rows // LANES, cells // HALO - 2),
        in_specs=[field_spec, field_spec],
        out_specs=out_spec,
        out_shape=jax.ShapeDtypeStruct(base_flow.shape, jnp.float32),
    )(base_flow, adjoint)


def boundary_kernel(base_ref, adj_ref, tail_ref, head_ref, prev_ref, out_ref, ext_ref):
    comps, cells, span, rows = base_ref.shape
    side = pl.program_id(0)

    @pl.when(side == 0)
    def _():
        ext_ref[0, :, HALO : HALO + cells] = base_ref[...]
        ext_ref[1, :, HALO : HALO + cells] = adj_ref[...]
        ext_ref[:, :, :HALO] = tail_ref[...]
        ext_ref[:, :, HALO + cells :] = head_ref[...]

    first = side * (cells - HALO)
    for lane in range(rows // LANES):
        lanes = pl.ds(lane * LANES, LANES)

        def load(field, c, x, lanes=lanes):
            return ext_ref[field, c, x + HALO, :, lanes]

        def step(i, carry, lanes=lanes, load=load):
            def write(c, value):
                out_ref[c, i, :, lanes] = value

            cell_update(load, first + i, write)
            return carry

        lax.fori_loop(0, HALO, step, 0)


def boundary_update(base_flow, adjoint, tails, heads, previous):
    comps, cells, span, rows = base_flow.shape
    full_spec = pl.BlockSpec((comps, cells, span, rows), lambda s: (0, 0, 0, 0))
    halo_spec = pl.BlockSpec((2, comps, HALO, span, rows), lambda s: (0, 0, 0, 0, 0))
    out_spec = pl.BlockSpec((comps, HALO, span, rows), lambda s: (0, s * (cells // HALO - 1), 0, 0))
    return pl.pallas_call(
        boundary_kernel,
        grid=(2,),
        in_specs=[full_spec, full_spec, halo_spec, halo_spec, pl.BlockSpec(memory_space=pl.ANY)],
        out_specs=out_spec,
        out_shape=jax.ShapeDtypeStruct(base_flow.shape, jnp.float32),
        scratch_shapes=[pltpu.VMEM((2, comps, cells + 2 * HALO, span, rows), jnp.float32)],
        input_output_aliases={4: 0},
    )(base_flow, adjoint, tails, heads, previous)


def side_kernel(side_ref, base_ref, adj_ref, halo_ref, prev_ref, out_ref, ext_ref):
    comps, near, span, rows = base_ref.shape

    @pl.when(side_ref[0] == 0)
    def _():
        ext_ref[:, :, :HALO] = halo_ref[...]
        ext_ref[0, :, HALO:] = base_ref[...]
        ext_ref[1, :, HALO:] = adj_ref[...]

    @pl.when(side_ref[0] != 0)
    def _():
        ext_ref[0, :, :near] = base_ref[...]
        ext_ref[1, :, :near] = adj_ref[...]
        ext_ref[:, :, near:] = halo_ref[...]

    for lane in range(rows // LANES):
        lanes = pl.ds(lane * LANES, LANES)

        def load(field, c, x, lanes=lanes):
            return ext_ref[field, c, x, :, lanes]

        def step(i, carry, lanes=lanes, load=load):
            def write(c, value):
                out_ref[c, i, :, lanes] = value

            cell_update(load, HALO + i, write)
            return carry

        lax.fori_loop(0, HALO, step, 0)


def side_update(base_flow, adjoint, halo, side, previous):
    comps, cells, span, rows = base_flow.shape
    near = 2 * HALO
    last = cells // near - 1
    body_spec = pl.BlockSpec((comps, near, span, rows), lambda i, side_ref: (0, side_ref[0] * last, 0, 0))
    halo_spec = pl.BlockSpec((2, comps, HALO, span, rows), lambda i, side_ref: (0, 0, 0, 0, 0))
    out_spec = pl.BlockSpec(
        (comps, HALO, span, rows), lambda i, side_ref: (0, side_ref[0] * (cells // HALO - 1), 0, 0)
    )
    grid_spec = pltpu.PrefetchScalarGridSpec(
        num_scalar_prefetch=1,
        grid=(1,),
        in_specs=[body_spec, body_spec, halo_spec, pl.BlockSpec(memory_space=pl.ANY)],
        out_specs=out_spec,
        scratch_shapes=[pltpu.VMEM((2, comps, near + HALO, span, rows), jnp.float32)],
    )
    return pl.pallas_call(
        side_kernel,
        grid_spec=grid_spec,
        out_shape=jax.ShapeDtypeStruct(base_flow.shape, jnp.float32),
        input_output_aliases={4: 0},
    )(side, base_flow, adjoint, halo, previous)


def body(base_flow, adjoint, first_op, second_op, far=()):
    comps, cells, spanwise, local_rows = base_flow.shape
    groups = lax.axis_size("gy")
    total_rows = local_rows * groups
    part = spanwise // groups

    base_low = lax.optimization_barrier(base_flow.astype(jnp.bfloat16))
    adjoint_low = lax.optimization_barrier(adjoint.astype(jnp.bfloat16))
    low = jnp.concatenate((base_low, adjoint_low), 0).reshape(2 * comps, cells, spanwise, 1, local_rows)
    lines = lax.all_to_all(low, "gy", split_axis=2, concat_axis=3, tiled=True)
    tail_cells = jnp.stack((base_flow[:, cells - HALO :], adjoint[:, cells - HALO :]), 0)
    head_cells = jnp.stack((base_flow[:, :HALO], adjoint[:, :HALO]), 0)
    tails = ring_shift(tail_cells, "gx", True, far, False)
    heads = ring_shift(head_cells, "gx", False, far, False)
    far_pairs, sends_tail, gets_tail = far_plan(far)
    far_send = jnp.where(sends_tail, tail_cells, head_cells)
    partial = interior_update(base_flow, adjoint)
    partial, far_send = lax.optimization_barrier((partial, far_send))
    received = lax.ppermute(far_send, "gx", far_pairs)
    lines, partial, tails, heads = lax.optimization_barrier((lines, partial, tails, heads))
    far_side = jnp.where(sends_tail, 1, 0).astype(jnp.int32).reshape(1)
    side_halo = jnp.where(gets_tail | sends_tail, received, tails)
    lines = lines.reshape(2 * comps, cells, part, total_rows)
    base_lines = lines[:comps]
    adj_lines = lines[comps:]
    slope_base = jnp.einsum("fxzk,ik->fxzi", base_lines, first_op, preferred_element_type=jnp.float32)
    slope_adj = jnp.einsum("fxzk,ik->fxzi", adj_lines, first_op, preferred_element_type=jnp.float32)
    curves = jnp.einsum("fxzk,ik->fxzi", adj_lines, second_op, preferred_element_type=jnp.float32)
    normal_vel = base_lines[1].astype(jnp.float32)
    coupling = jnp.sum(adj_lines.astype(jnp.float32) * slope_base, axis=0)
    wall_part = normal_vel[None] * slope_adj + VISCOSITY * curves
    wall_part = wall_part.at[1].add(-coupling)
    wall_part = wall_part.astype(jnp.bfloat16).reshape(comps, cells, part, groups, local_rows)
    wall_part, partial = lax.optimization_barrier((wall_part, partial))
    wall_part = lax.all_to_all(wall_part, "gy", split_axis=3, concat_axis=2, tiled=True)
    wall_part = wall_part.reshape(comps, cells, spanwise, local_rows).astype(jnp.float32)

    partial = boundary_update(base_flow, adjoint, tails, heads, partial)
    partial = side_update(base_flow, adjoint, side_halo, far_side, partial)
    updated = partial + STEP_WEIGHT * wall_part
    wall_index = lax.axis_index("gy") * local_rows + jnp.arange(local_rows, dtype=jnp.int32)
    interior = (wall_index > 0) & (wall_index < total_rows - 1)
    return jnp.where(interior, updated, jnp.float32(0.0))


def far_plan(far):
    count = lax.axis_size("gx")
    links = [i for i in range(count) if far[i]]
    tail_senders = {i for i in links}
    head_senders = {(i + 1) % count for i in links}
    assert links and not (tail_senders & head_senders)
    pairs = [(i, (i + 1) % count) for i in links] + [((i + 1) % count, i) for i in links]
    position = lax.axis_index("gx")
    sends_tail = jnp.zeros((), jnp.bool_)
    gets_tail = jnp.zeros((), jnp.bool_)
    for i in links:
        sends_tail = sends_tail | (position == i)
        gets_tail = gets_tail | (position == (i + 1) % count)
    return pairs, sends_tail, gets_tail


def far_links(mesh):
    devices = mesh.devices
    count = devices.shape[0]
    return tuple(
        bool(devices[i, 0].coords[1] != devices[(i + 1) % count, 0].coords[1]) for i in range(count)
    )


def solution(mesh):
    return jax.shard_map(
        functools.partial(body, far=far_links(mesh)),
        mesh=mesh,
        in_specs=(P(None, "gx", None, "gy"), P(None, "gx", None, "gy"), P(), P()),
        out_specs=P(None, "gx", None, "gy"),
        check_vma=False,
    )
```

```python
import functools

import jax
import jax.numpy as jnp
from jax import lax
from jax.experimental import pallas as pl
from jax.experimental.pallas import tpu as pltpu
from jax.sharding import PartitionSpec as P

C_FIRST = (0.8, -0.2, 4.0 / 105.0, -1.0 / 280.0)
C_SECOND = (1.6, -0.2, 8.0 / 315.0, -1.0 / 560.0)
C_CENTER = -205.0 / 72.0
VISCOSITY = 0.1
STEP_WEIGHT = 0.5
HALO = 4
LANES = 128


def ring_shift(value, axis, forward, far, want_far):
    count = lax.axis_size(axis)
    links = [i for i in range(count) if far[i] == want_far]
    if forward:
        pairs = [(i, (i + 1) % count) for i in links]
    else:
        pairs = [((i + 1) % count, i) for i in links]
    return lax.ppermute(value, axis, pairs)


def cell_update(load, x, write):
    span = load(0, 0, x).shape[0]

    def zshift(v, k):
        return pltpu.roll(v, (span - k) % span, 0)

    def derivs(field, c, second):
        center = load(field, c, x)
        plus = [load(field, c, x + k) for k in range(1, 5)]
        minus = [load(field, c, x - k) for k in range(1, 5)]
        zp = [zshift(center, k) for k in range(1, 5)]
        zm = [zshift(center, span - k) for k in range(1, 5)]
        dx = C_FIRST[0] * (plus[0] - minus[0])
        dz = C_FIRST[0] * (zp[0] - zm[0])
        for k in range(1, 4):
            dx = dx + C_FIRST[k] * (plus[k] - minus[k])
            dz = dz + C_FIRST[k] * (zp[k] - zm[k])
        if not second:
            return center, dx, dz, None, None
        dxx = C_CENTER * center
        dzz = C_CENTER * center
        for k in range(4):
            dxx = dxx + C_SECOND[k] * (plus[k] + minus[k])
            dzz = dzz + C_SECOND[k] * (zp[k] + zm[k])
        return center, dx, dz, dxx, dzz

    base = [derivs(0, j, False) for j in range(3)]
    adj = [derivs(1, c, True) for c in range(3)]
    first_coupling = adj[0][0] * base[0][1] + adj[1][0] * base[1][1] + adj[2][0] * base[2][1]
    last_coupling = adj[0][0] * base[0][2] + adj[1][0] * base[1][2] + adj[2][0] * base[2][2]
    for c in range(3):
        center, dx, dz, dxx, dzz = adj[c]
        tendency = base[0][0] * dx + base[2][0] * dz + VISCOSITY * (dxx + dzz)
        if c == 0:
            tendency = tendency - first_coupling
        elif c == 2:
            tendency = tendency - last_coupling
        write(c, center + STEP_WEIGHT * tendency)


def interior_kernel(base_ref, adj_ref, out_ref):
    first = (pl.program_id(1) + 1) * HALO

    def load(field, c, x):
        return (base_ref if field == 0 else adj_ref)[c, x]

    def step(i, carry):
        def write(c, value):
            out_ref[c, i] = value

        cell_update(load, first + i, write)
        return carry

    lax.fori_loop(0, HALO, step, 0)


def interior_update(base_flow, adjoint):
    comps, cells, span, rows = base_flow.shape
    field_spec = pl.BlockSpec((comps, cells, span, LANES), lambda j, b: (0, 0, 0, j))
    out_spec = pl.BlockSpec((comps, HALO, span, LANES), lambda j, b: (0, b + 1, 0, j))
    return pl.pallas_call(
        interior_kernel,
        grid=(rows // LANES, cells // HALO - 2),
        in_specs=[field_spec, field_spec],
        out_specs=out_spec,
        out_shape=jax.ShapeDtypeStruct(base_flow.shape, jnp.float32),
    )(base_flow, adjoint)


def boundary_kernel(base_ref, adj_ref, tail_ref, head_ref, prev_ref, out_ref, ext_ref):
    comps, cells, span, rows = base_ref.shape
    side = pl.program_id(0)

    @pl.when(side == 0)
    def _():
        ext_ref[0, :, HALO : HALO + cells] = base_ref[...]
        ext_ref[1, :, HALO : HALO + cells] = adj_ref[...]
        ext_ref[:, :, :HALO] = tail_ref[...]
        ext_ref[:, :, HALO + cells :] = head_ref[...]

    first = side * (cells - HALO)
    for lane in range(rows // LANES):
        lanes = pl.ds(lane * LANES, LANES)

        def load(field, c, x, lanes=lanes):
            return ext_ref[field, c, x + HALO, :, lanes]

        def step(i, carry, lanes=lanes, load=load):
            def write(c, value):
                out_ref[c, i, :, lanes] = value

            cell_update(load, first + i, write)
            return carry

        lax.fori_loop(0, HALO, step, 0)


def boundary_update(base_flow, adjoint, tails, heads, previous):
    comps, cells, span, rows = base_flow.shape
    full_spec = pl.BlockSpec((comps, cells, span, rows), lambda s: (0, 0, 0, 0))
    halo_spec = pl.BlockSpec((2, comps, HALO, span, rows), lambda s: (0, 0, 0, 0, 0))
    out_spec = pl.BlockSpec((comps, HALO, span, rows), lambda s: (0, s * (cells // HALO - 1), 0, 0))
    return pl.pallas_call(
        boundary_kernel,
        grid=(2,),
        in_specs=[full_spec, full_spec, halo_spec, halo_spec, pl.BlockSpec(memory_space=pl.ANY)],
        out_specs=out_spec,
        out_shape=jax.ShapeDtypeStruct(base_flow.shape, jnp.float32),
        scratch_shapes=[pltpu.VMEM((2, comps, cells + 2 * HALO, span, rows), jnp.float32)],
        input_output_aliases={4: 0},
    )(base_flow, adjoint, tails, heads, previous)


def side_kernel(side_ref, base_ref, adj_ref, halo_ref, prev_ref, out_ref, ext_ref):
    comps, near, span, rows = base_ref.shape

    @pl.when(side_ref[0] == 0)
    def _():
        ext_ref[:, :, :HALO] = halo_ref[...]
        ext_ref[0, :, HALO:] = base_ref[...]
        ext_ref[1, :, HALO:] = adj_ref[...]

    @pl.when(side_ref[0] != 0)
    def _():
        ext_ref[0, :, :near] = base_ref[...]
        ext_ref[1, :, :near] = adj_ref[...]
        ext_ref[:, :, near:] = halo_ref[...]

    for lane in range(rows // LANES):
        lanes = pl.ds(lane * LANES, LANES)

        def load(field, c, x, lanes=lanes):
            return ext_ref[field, c, x, :, lanes]

        def step(i, carry, lanes=lanes, load=load):
            def write(c, value):
                out_ref[c, i, :, lanes] = value

            cell_update(load, HALO + i, write)
            return carry

        lax.fori_loop(0, HALO, step, 0)


def side_update(base_flow, adjoint, halo, side, previous):
    comps, cells, span, rows = base_flow.shape
    near = 2 * HALO
    last = cells // near - 1
    body_spec = pl.BlockSpec((comps, near, span, rows), lambda i, side_ref: (0, side_ref[0] * last, 0, 0))
    halo_spec = pl.BlockSpec((2, comps, HALO, span, rows), lambda i, side_ref: (0, 0, 0, 0, 0))
    out_spec = pl.BlockSpec(
        (comps, HALO, span, rows), lambda i, side_ref: (0, side_ref[0] * (cells // HALO - 1), 0, 0)
    )
    grid_spec = pltpu.PrefetchScalarGridSpec(
        num_scalar_prefetch=1,
        grid=(1,),
        in_specs=[body_spec, body_spec, halo_spec, pl.BlockSpec(memory_space=pl.ANY)],
        out_specs=out_spec,
        scratch_shapes=[pltpu.VMEM((2, comps, near + HALO, span, rows), jnp.float32)],
    )
    return pl.pallas_call(
        side_kernel,
        grid_spec=grid_spec,
        out_shape=jax.ShapeDtypeStruct(base_flow.shape, jnp.float32),
        input_output_aliases={4: 0},
    )(side, base_flow, adjoint, halo, previous)


def body(base_flow, adjoint, first_op, second_op, far=()):
    comps, cells, spanwise, local_rows = base_flow.shape
    groups = lax.axis_size("gy")
    total_rows = local_rows * groups
    part = spanwise // groups

    base_low = lax.optimization_barrier(base_flow.astype(jnp.bfloat16))
    adjoint_low = lax.optimization_barrier(adjoint.astype(jnp.bfloat16))
    low = jnp.concatenate((base_low, adjoint_low), 0).reshape(2 * comps, cells, spanwise, 1, local_rows)
    lines = lax.all_to_all(low, "gy", split_axis=2, concat_axis=3, tiled=True)
    tail_cells = jnp.stack((base_flow[:, cells - HALO :], adjoint[:, cells - HALO :]), 0)
    head_cells = jnp.stack((base_flow[:, :HALO], adjoint[:, :HALO]), 0)
    tails = ring_shift(tail_cells, "gx", True, far, False)
    heads = ring_shift(head_cells, "gx", False, far, False)
    count = lax.axis_size("gx")
    far_all = [i for i in range(count) if far[i]]
    assert far_all
    early_links = [i for i in far_all if i != count - 1]
    late_links = [i for i in far_all if i == count - 1]
    _, sends_tail, gets_tail = far_plan(far_all)
    far_send = jnp.where(sends_tail, tail_cells, head_cells)
    partial = interior_update(base_flow, adjoint)
    partial, far_send = lax.optimization_barrier((partial, far_send))
    received = jnp.zeros_like(far_send)
    if early_links:
        received = lax.ppermute(far_send, "gx", far_plan(early_links)[0])
    lines, partial, tails, heads, far_send = lax.optimization_barrier((lines, partial, tails, heads, far_send))
    if late_links:
        received = received + lax.ppermute(far_send, "gx", far_plan(late_links)[0])
    far_side = jnp.where(sends_tail, 1, 0).astype(jnp.int32).reshape(1)
    side_halo = jnp.where(gets_tail | sends_tail, received, tails)
    lines = lines.reshape(2 * comps, cells, part, total_rows)
    base_lines = lines[:comps]
    adj_lines = lines[comps:]
    slope_base = jnp.einsum("fxzk,ik->fxzi", base_lines, first_op, preferred_element_type=jnp.float32)
    slope_adj = jnp.einsum("fxzk,ik->fxzi", adj_lines, first_op, preferred_element_type=jnp.float32)
    curves = jnp.einsum("fxzk,ik->fxzi", adj_lines, second_op, preferred_element_type=jnp.float32)
    normal_vel = base_lines[1].astype(jnp.float32)
    coupling = jnp.sum(adj_lines.astype(jnp.float32) * slope_base, axis=0)
    wall_part = normal_vel[None] * slope_adj + VISCOSITY * curves
    wall_part = wall_part.at[1].add(-coupling)
    wall_part = wall_part.astype(jnp.bfloat16).reshape(comps, cells, part, groups, local_rows)
    wall_part, partial = lax.optimization_barrier((wall_part, partial))
    wall_part = lax.all_to_all(wall_part, "gy", split_axis=3, concat_axis=2, tiled=True)
    wall_part = wall_part.reshape(comps, cells, spanwise, local_rows).astype(jnp.float32)

    partial = boundary_update(base_flow, adjoint, tails, heads, partial)
    partial = side_update(base_flow, adjoint, side_halo, far_side, partial)
    updated = partial + STEP_WEIGHT * wall_part
    wall_index = lax.axis_index("gy") * local_rows + jnp.arange(local_rows, dtype=jnp.int32)
    interior = (wall_index > 0) & (wall_index < total_rows - 1)
    return jnp.where(interior, updated, jnp.float32(0.0))


def far_plan(links):
    count = lax.axis_size("gx")
    tail_senders = {i for i in links}
    head_senders = {(i + 1) % count for i in links}
    assert not (tail_senders & head_senders)
    pairs = [(i, (i + 1) % count) for i in links] + [((i + 1) % count, i) for i in links]
    position = lax.axis_index("gx")
    sends_tail = jnp.zeros((), jnp.bool_)
    gets_tail = jnp.zeros((), jnp.bool_)
    for i in links:
        sends_tail = sends_tail | (position == i)
        gets_tail = gets_tail | (position == (i + 1) % count)
    return pairs, sends_tail, gets_tail


def far_links(mesh):
    devices = mesh.devices
    count = devices.shape[0]
    return tuple(
        bool(devices[i, 0].coords[1] != devices[(i + 1) % count, 0].coords[1]) for i in range(count)
    )


def solution(mesh):
    return jax.shard_map(
        functools.partial(body, far=far_links(mesh)),
        mesh=mesh,
        in_specs=(P(None, "gx", None, "gy"), P(None, "gx", None, "gy"), P(), P()),
        out_specs=P(None, "gx", None, "gy"),
        check_vma=False,
    )
```

```python
import functools

import jax
import jax.numpy as jnp
from jax import lax
from jax.experimental import pallas as pl
from jax.experimental.pallas import tpu as pltpu
from jax.sharding import PartitionSpec as P

C_FIRST = (0.8, -0.2, 4.0 / 105.0, -1.0 / 280.0)
C_SECOND = (1.6, -0.2, 8.0 / 315.0, -1.0 / 560.0)
C_CENTER = -205.0 / 72.0
VISCOSITY = 0.1
STEP_WEIGHT = 0.5
HALO = 4
LANES = 128


def ring_shift(value, axis, forward, far, want_far):
    count = lax.axis_size(axis)
    links = [i for i in range(count) if far[i] == want_far]
    if forward:
        pairs = [(i, (i + 1) % count) for i in links]
    else:
        pairs = [((i + 1) % count, i) for i in links]
    return lax.ppermute(value, axis, pairs)


def cell_update(load, x, write):
    span = load(0, 0, x).shape[0]

    def zshift(v, k):
        return pltpu.roll(v, (span - k) % span, 0)

    def derivs(field, c, second):
        center = load(field, c, x)
        plus = [load(field, c, x + k) for k in range(1, 5)]
        minus = [load(field, c, x - k) for k in range(1, 5)]
        zp = [zshift(center, k) for k in range(1, 5)]
        zm = [zshift(center, span - k) for k in range(1, 5)]
        dx = C_FIRST[0] * (plus[0] - minus[0])
        dz = C_FIRST[0] * (zp[0] - zm[0])
        for k in range(1, 4):
            dx = dx + C_FIRST[k] * (plus[k] - minus[k])
            dz = dz + C_FIRST[k] * (zp[k] - zm[k])
        if not second:
            return center, dx, dz, None, None
        dxx = C_CENTER * center
        dzz = C_CENTER * center
        for k in range(4):
            dxx = dxx + C_SECOND[k] * (plus[k] + minus[k])
            dzz = dzz + C_SECOND[k] * (zp[k] + zm[k])
        return center, dx, dz, dxx, dzz

    base = [derivs(0, j, False) for j in range(3)]
    adj = [derivs(1, c, True) for c in range(3)]
    first_coupling = adj[0][0] * base[0][1] + adj[1][0] * base[1][1] + adj[2][0] * base[2][1]
    last_coupling = adj[0][0] * base[0][2] + adj[1][0] * base[1][2] + adj[2][0] * base[2][2]
    for c in range(3):
        center, dx, dz, dxx, dzz = adj[c]
        tendency = base[0][0] * dx + base[2][0] * dz + VISCOSITY * (dxx + dzz)
        if c == 0:
            tendency = tendency - first_coupling
        elif c == 2:
            tendency = tendency - last_coupling
        write(c, center + STEP_WEIGHT * tendency)


def interior_kernel(base_ref, adj_ref, out_ref):
    first = (pl.program_id(1) + 1) * HALO

    def load(field, c, x):
        return (base_ref if field == 0 else adj_ref)[c, x]

    def step(i, carry):
        def write(c, value):
            out_ref[c, i] = value

        cell_update(load, first + i, write)
        return carry

    lax.fori_loop(0, HALO, step, 0)


def interior_update(base_flow, adjoint):
    comps, cells, span, rows = base_flow.shape
    field_spec = pl.BlockSpec((comps, cells, span, LANES), lambda j, b: (0, 0, 0, j))
    out_spec = pl.BlockSpec((comps, HALO, span, LANES), lambda j, b: (0, b + 1, 0, j))
    return pl.pallas_call(
        interior_kernel,
        grid=(rows // LANES, cells // HALO - 2),
        in_specs=[field_spec, field_spec],
        out_specs=out_spec,
        out_shape=jax.ShapeDtypeStruct(base_flow.shape, jnp.float32),
    )(base_flow, adjoint)


def boundary_kernel(base_ref, adj_ref, tail_ref, head_ref, prev_ref, out_ref, ext_ref):
    comps, cells, span, rows = base_ref.shape
    side = pl.program_id(0)

    @pl.when(side == 0)
    def _():
        ext_ref[0, :, HALO : HALO + cells] = base_ref[...]
        ext_ref[1, :, HALO : HALO + cells] = adj_ref[...]
        ext_ref[:, :, :HALO] = tail_ref[...]
        ext_ref[:, :, HALO + cells :] = head_ref[...]

    first = side * (cells - HALO)
    for lane in range(rows // LANES):
        lanes = pl.ds(lane * LANES, LANES)

        def load(field, c, x, lanes=lanes):
            return ext_ref[field, c, x + HALO, :, lanes]

        def step(i, carry, lanes=lanes, load=load):
            def write(c, value):
                out_ref[c, i, :, lanes] = value

            cell_update(load, first + i, write)
            return carry

        lax.fori_loop(0, HALO, step, 0)


def boundary_update(base_flow, adjoint, tails, heads, previous):
    comps, cells, span, rows = base_flow.shape
    full_spec = pl.BlockSpec((comps, cells, span, rows), lambda s: (0, 0, 0, 0))
    halo_spec = pl.BlockSpec((2, comps, HALO, span, rows), lambda s: (0, 0, 0, 0, 0))
    out_spec = pl.BlockSpec((comps, HALO, span, rows), lambda s: (0, s * (cells // HALO - 1), 0, 0))
    return pl.pallas_call(
        boundary_kernel,
        grid=(2,),
        in_specs=[full_spec, full_spec, halo_spec, halo_spec, pl.BlockSpec(memory_space=pl.ANY)],
        out_specs=out_spec,
        out_shape=jax.ShapeDtypeStruct(base_flow.shape, jnp.float32),
        scratch_shapes=[pltpu.VMEM((2, comps, cells + 2 * HALO, span, rows), jnp.float32)],
        input_output_aliases={4: 0},
    )(base_flow, adjoint, tails, heads, previous)


def side_kernel(side_ref, base_ref, adj_ref, halo_ref, prev_ref, out_ref, ext_ref):
    comps, near, span, rows = base_ref.shape

    @pl.when(side_ref[0] == 0)
    def _():
        ext_ref[:, :, :HALO] = halo_ref[...]
        ext_ref[0, :, HALO:] = base_ref[...]
        ext_ref[1, :, HALO:] = adj_ref[...]

    @pl.when(side_ref[0] != 0)
    def _():
        ext_ref[0, :, :near] = base_ref[...]
        ext_ref[1, :, :near] = adj_ref[...]
        ext_ref[:, :, near:] = halo_ref[...]

    for lane in range(rows // LANES):
        lanes = pl.ds(lane * LANES, LANES)

        def load(field, c, x, lanes=lanes):
            return ext_ref[field, c, x, :, lanes]

        def step(i, carry, lanes=lanes, load=load):
            def write(c, value):
                out_ref[c, i, :, lanes] = value

            cell_update(load, HALO + i, write)
            return carry

        lax.fori_loop(0, HALO, step, 0)


def side_update(base_flow, adjoint, halo, side, previous):
    comps, cells, span, rows = base_flow.shape
    near = 2 * HALO
    last = cells // near - 1
    body_spec = pl.BlockSpec((comps, near, span, rows), lambda i, side_ref: (0, side_ref[0] * last, 0, 0))
    halo_spec = pl.BlockSpec((2, comps, HALO, span, rows), lambda i, side_ref: (0, 0, 0, 0, 0))
    out_spec = pl.BlockSpec(
        (comps, HALO, span, rows), lambda i, side_ref: (0, side_ref[0] * (cells // HALO - 1), 0, 0)
    )
    grid_spec = pltpu.PrefetchScalarGridSpec(
        num_scalar_prefetch=1,
        grid=(1,),
        in_specs=[body_spec, body_spec, halo_spec, pl.BlockSpec(memory_space=pl.ANY)],
        out_specs=out_spec,
        scratch_shapes=[pltpu.VMEM((2, comps, near + HALO, span, rows), jnp.float32)],
    )
    return pl.pallas_call(
        side_kernel,
        grid_spec=grid_spec,
        out_shape=jax.ShapeDtypeStruct(base_flow.shape, jnp.float32),
        input_output_aliases={4: 0},
    )(side, base_flow, adjoint, halo, previous)


def body(base_flow, adjoint, first_op, second_op, far=()):
    comps, cells, spanwise, local_rows = base_flow.shape
    groups = lax.axis_size("gy")
    total_rows = local_rows * groups
    part = spanwise // groups

    base_low = lax.optimization_barrier(base_flow.astype(jnp.bfloat16))
    adjoint_low = lax.optimization_barrier(adjoint.astype(jnp.bfloat16))
    low = jnp.concatenate((base_low, adjoint_low), 0).reshape(2 * comps, cells, spanwise, 1, local_rows)
    lines = lax.all_to_all(low, "gy", split_axis=2, concat_axis=3, tiled=True)
    tail_cells = jnp.stack((base_flow[:, cells - HALO :], adjoint[:, cells - HALO :]), 0)
    head_cells = jnp.stack((base_flow[:, :HALO], adjoint[:, :HALO]), 0)
    tails = ring_shift(tail_cells, "gx", True, far, False)
    heads = ring_shift(head_cells, "gx", False, far, False)
    far_pairs, sends_tail, gets_tail = far_plan(far)
    far_send = jnp.where(sends_tail, tail_cells, head_cells)
    partial = interior_update(base_flow, adjoint)
    lines, partial, tails, heads, far_send = lax.optimization_barrier((lines, partial, tails, heads, far_send))
    lines = lines.reshape(2 * comps, cells, part, total_rows)
    base_lines = lines[:comps]
    adj_lines = lines[comps:]
    slope_base = jnp.einsum("fxzk,ik->fxzi", base_lines, first_op, preferred_element_type=jnp.float32)
    slope_base, far_send = lax.optimization_barrier((slope_base, far_send))
    received = lax.ppermute(far_send, "gx", far_pairs)
    far_side = jnp.where(sends_tail, 1, 0).astype(jnp.int32).reshape(1)
    side_halo = jnp.where(gets_tail | sends_tail, received, tails)
    slope_adj = jnp.einsum("fxzk,ik->fxzi", adj_lines, first_op, preferred_element_type=jnp.float32)
    curves = jnp.einsum("fxzk,ik->fxzi", adj_lines, second_op, preferred_element_type=jnp.float32)
    normal_vel = base_lines[1].astype(jnp.float32)
    coupling = jnp.sum(adj_lines.astype(jnp.float32) * slope_base, axis=0)
    wall_part = normal_vel[None] * slope_adj + VISCOSITY * curves
    wall_part = wall_part.at[1].add(-coupling)
    wall_part = wall_part.astype(jnp.bfloat16).reshape(comps, cells, part, groups, local_rows)
    wall_part, partial = lax.optimization_barrier((wall_part, partial))
    wall_part = lax.all_to_all(wall_part, "gy", split_axis=3, concat_axis=2, tiled=True)
    wall_part = wall_part.reshape(comps, cells, spanwise, local_rows).astype(jnp.float32)

    partial = boundary_update(base_flow, adjoint, tails, heads, partial)
    partial = side_update(base_flow, adjoint, side_halo, far_side, partial)
    updated = partial + STEP_WEIGHT * wall_part
    wall_index = lax.axis_index("gy") * local_rows + jnp.arange(local_rows, dtype=jnp.int32)
    interior = (wall_index > 0) & (wall_index < total_rows - 1)
    return jnp.where(interior, updated, jnp.float32(0.0))


def far_plan(far):
    count = lax.axis_size("gx")
    links = [i for i in range(count) if far[i]]
    tail_senders = {i for i in links}
    head_senders = {(i + 1) % count for i in links}
    assert links and not (tail_senders & head_senders)
    pairs = [(i, (i + 1) % count) for i in links] + [((i + 1) % count, i) for i in links]
    position = lax.axis_index("gx")
    sends_tail = jnp.zeros((), jnp.bool_)
    gets_tail = jnp.zeros((), jnp.bool_)
    for i in links:
        sends_tail = sends_tail | (position == i)
        gets_tail = gets_tail | (position == (i + 1) % count)
    return pairs, sends_tail, gets_tail


def far_links(mesh):
    devices = mesh.devices
    count = devices.shape[0]
    return tuple(
        bool(devices[i, 0].coords[1] != devices[(i + 1) % count, 0].coords[1]) for i in range(count)
    )


def solution(mesh):
    return jax.shard_map(
        functools.partial(body, far=far_links(mesh)),
        mesh=mesh,
        in_specs=(P(None, "gx", None, "gy"), P(None, "gx", None, "gy"), P(), P()),
        out_specs=P(None, "gx", None, "gy"),
        check_vma=False,
    )
```

```python
import functools

import jax
import jax.numpy as jnp
from jax import lax
from jax.experimental import pallas as pl
from jax.experimental.pallas import tpu as pltpu
from jax.sharding import PartitionSpec as P

C_FIRST = (0.8, -0.2, 4.0 / 105.0, -1.0 / 280.0)
C_SECOND = (1.6, -0.2, 8.0 / 315.0, -1.0 / 560.0)
C_CENTER = -205.0 / 72.0
VISCOSITY = 0.1
STEP_WEIGHT = 0.5
HALO = 4
LANES = 128


def ring_shift(value, axis, forward, far, want_far):
    count = lax.axis_size(axis)
    links = [i for i in range(count) if far[i] == want_far]
    if forward:
        pairs = [(i, (i + 1) % count) for i in links]
    else:
        pairs = [((i + 1) % count, i) for i in links]
    return lax.ppermute(value, axis, pairs)


def cell_update(load, x, write):
    span = load(0, 0, x).shape[0]

    def zshift(v, k):
        return pltpu.roll(v, (span - k) % span, 0)

    def derivs(field, c, second):
        center = load(field, c, x)
        plus = [load(field, c, x + k) for k in range(1, 5)]
        minus = [load(field, c, x - k) for k in range(1, 5)]
        zp = [zshift(center, k) for k in range(1, 5)]
        zm = [zshift(center, span - k) for k in range(1, 5)]
        dx = C_FIRST[0] * (plus[0] - minus[0])
        dz = C_FIRST[0] * (zp[0] - zm[0])
        for k in range(1, 4):
            dx = dx + C_FIRST[k] * (plus[k] - minus[k])
            dz = dz + C_FIRST[k] * (zp[k] - zm[k])
        if not second:
            return center, dx, dz, None, None
        dxx = C_CENTER * center
        dzz = C_CENTER * center
        for k in range(4):
            dxx = dxx + C_SECOND[k] * (plus[k] + minus[k])
            dzz = dzz + C_SECOND[k] * (zp[k] + zm[k])
        return center, dx, dz, dxx, dzz

    base = [derivs(0, j, False) for j in range(3)]
    adj = [derivs(1, c, True) for c in range(3)]
    first_coupling = adj[0][0] * base[0][1] + adj[1][0] * base[1][1] + adj[2][0] * base[2][1]
    last_coupling = adj[0][0] * base[0][2] + adj[1][0] * base[1][2] + adj[2][0] * base[2][2]
    for c in range(3):
        center, dx, dz, dxx, dzz = adj[c]
        tendency = base[0][0] * dx + base[2][0] * dz + VISCOSITY * (dxx + dzz)
        if c == 0:
            tendency = tendency - first_coupling
        elif c == 2:
            tendency = tendency - last_coupling
        write(c, center + STEP_WEIGHT * tendency)


def interior_kernel(base_ref, adj_ref, out_ref):
    first = (pl.program_id(1) + 1) * HALO

    def load(field, c, x):
        return (base_ref if field == 0 else adj_ref)[c, x]

    def step(i, carry):
        def write(c, value):
            out_ref[c, i] = value

        cell_update(load, first + i, write)
        return carry

    lax.fori_loop(0, HALO, step, 0)


def interior_update(base_flow, adjoint):
    comps, cells, span, rows = base_flow.shape
    field_spec = pl.BlockSpec((comps, cells, span, LANES), lambda j, b: (0, 0, 0, j))
    out_spec = pl.BlockSpec((comps, HALO, span, LANES), lambda j, b: (0, b + 1, 0, j))
    return pl.pallas_call(
        interior_kernel,
        grid=(rows // LANES, cells // HALO - 2),
        in_specs=[field_spec, field_spec],
        out_specs=out_spec,
        out_shape=jax.ShapeDtypeStruct(base_flow.shape, jnp.float32),
    )(base_flow, adjoint)


def boundary_kernel(base_ref, adj_ref, tail_ref, head_ref, prev_ref, out_ref, ext_ref):
    comps, cells, span, rows = base_ref.shape
    side = pl.program_id(0)

    @pl.when(side == 0)
    def _():
        ext_ref[0, :, HALO : HALO + cells] = base_ref[...]
        ext_ref[1, :, HALO : HALO + cells] = adj_ref[...]
        ext_ref[:, :, :HALO] = tail_ref[...]
        ext_ref[:, :, HALO + cells :] = head_ref[...]

    first = side * (cells - HALO)
    for lane in range(rows // LANES):
        lanes = pl.ds(lane * LANES, LANES)

        def load(field, c, x, lanes=lanes):
            return ext_ref[field, c, x + HALO, :, lanes]

        def step(i, carry, lanes=lanes, load=load):
            def write(c, value):
                out_ref[c, i, :, lanes] = value

            cell_update(load, first + i, write)
            return carry

        lax.fori_loop(0, HALO, step, 0)


def boundary_update(base_flow, adjoint, tails, heads, previous):
    comps, cells, span, rows = base_flow.shape
    full_spec = pl.BlockSpec((comps, cells, span, rows), lambda s: (0, 0, 0, 0))
    halo_spec = pl.BlockSpec((2, comps, HALO, span, rows), lambda s: (0, 0, 0, 0, 0))
    out_spec = pl.BlockSpec((comps, HALO, span, rows), lambda s: (0, s * (cells // HALO - 1), 0, 0))
    return pl.pallas_call(
        boundary_kernel,
        grid=(2,),
        in_specs=[full_spec, full_spec, halo_spec, halo_spec, pl.BlockSpec(memory_space=pl.ANY)],
        out_specs=out_spec,
        out_shape=jax.ShapeDtypeStruct(base_flow.shape, jnp.float32),
        scratch_shapes=[pltpu.VMEM((2, comps, cells + 2 * HALO, span, rows), jnp.float32)],
        input_output_aliases={4: 0},
    )(base_flow, adjoint, tails, heads, previous)


def side_kernel(side_ref, base_ref, adj_ref, halo_ref, prev_ref, out_ref, ext_ref):
    comps, near, span, rows = base_ref.shape

    @pl.when(side_ref[0] == 0)
    def _():
        ext_ref[:, :, :HALO] = halo_ref[...]
        ext_ref[0, :, HALO:] = base_ref[...]
        ext_ref[1, :, HALO:] = adj_ref[...]

    @pl.when(side_ref[0] != 0)
    def _():
        ext_ref[0, :, :near] = base_ref[...]
        ext_ref[1, :, :near] = adj_ref[...]
        ext_ref[:, :, near:] = halo_ref[...]

    for lane in range(rows // LANES):
        lanes = pl.ds(lane * LANES, LANES)

        def load(field, c, x, lanes=lanes):
            return ext_ref[field, c, x, :, lanes]

        def step(i, carry, lanes=lanes, load=load):
            def write(c, value):
                out_ref[c, i, :, lanes] = value

            cell_update(load, HALO + i, write)
            return carry

        lax.fori_loop(0, HALO, step, 0)


def side_update(base_flow, adjoint, halo, side, previous):
    comps, cells, span, rows = base_flow.shape
    near = 2 * HALO
    last = cells // near - 1
    body_spec = pl.BlockSpec((comps, near, span, rows), lambda i, side_ref: (0, side_ref[0] * last, 0, 0))
    halo_spec = pl.BlockSpec((2, comps, HALO, span, rows), lambda i, side_ref: (0, 0, 0, 0, 0))
    out_spec = pl.BlockSpec(
        (comps, HALO, span, rows), lambda i, side_ref: (0, side_ref[0] * (cells // HALO - 1), 0, 0)
    )
    grid_spec = pltpu.PrefetchScalarGridSpec(
        num_scalar_prefetch=1,
        grid=(1,),
        in_specs=[body_spec, body_spec, halo_spec, pl.BlockSpec(memory_space=pl.ANY)],
        out_specs=out_spec,
        scratch_shapes=[pltpu.VMEM((2, comps, near + HALO, span, rows), jnp.float32)],
    )
    return pl.pallas_call(
        side_kernel,
        grid_spec=grid_spec,
        out_shape=jax.ShapeDtypeStruct(base_flow.shape, jnp.float32),
        input_output_aliases={4: 0},
    )(side, base_flow, adjoint, halo, previous)


def body(base_flow, adjoint, first_op, second_op, far=()):
    comps, cells, spanwise, local_rows = base_flow.shape
    groups = lax.axis_size("gy")
    total_rows = local_rows * groups
    part = spanwise // groups

    base_low = lax.optimization_barrier(base_flow.astype(jnp.bfloat16))
    adjoint_low = lax.optimization_barrier(adjoint.astype(jnp.bfloat16))
    low = jnp.concatenate((base_low, adjoint_low), 0).reshape(2 * comps, cells, spanwise, 1, local_rows)
    lines = lax.all_to_all(low, "gy", split_axis=2, concat_axis=3, tiled=True)
    tail_cells = jnp.stack((base_flow[:, cells - HALO :], adjoint[:, cells - HALO :]), 0)
    head_cells = jnp.stack((base_flow[:, :HALO], adjoint[:, :HALO]), 0)
    tails = ring_shift(tail_cells, "gx", True, far, False)
    heads = ring_shift(head_cells, "gx", False, far, False)
    count = lax.axis_size("gx")
    far_all = [i for i in range(count) if far[i]]
    assert far_all
    early_links = [i for i in far_all if i == count - 1]
    late_links = [i for i in far_all if i != count - 1]
    _, sends_tail, gets_tail = far_plan(far_all)
    far_send = jnp.where(sends_tail, tail_cells, head_cells)
    partial = interior_update(base_flow, adjoint)
    partial, far_send = lax.optimization_barrier((partial, far_send))
    received = jnp.zeros_like(far_send)
    if early_links:
        received = lax.ppermute(far_send, "gx", far_plan(early_links)[0])
    lines, partial, tails, heads, far_send = lax.optimization_barrier((lines, partial, tails, heads, far_send))
    if late_links:
        received = received + lax.ppermute(far_send, "gx", far_plan(late_links)[0])
    far_side = jnp.where(sends_tail, 1, 0).astype(jnp.int32).reshape(1)
    side_halo = jnp.where(gets_tail | sends_tail, received, tails)
    lines = lines.reshape(2 * comps, cells, part, total_rows)
    base_lines = lines[:comps]
    adj_lines = lines[comps:]
    slope_base = jnp.einsum("fxzk,ik->fxzi", base_lines, first_op, preferred_element_type=jnp.float32)
    slope_adj = jnp.einsum("fxzk,ik->fxzi", adj_lines, first_op, preferred_element_type=jnp.float32)
    curves = jnp.einsum("fxzk,ik->fxzi", adj_lines, second_op, preferred_element_type=jnp.float32)
    normal_vel = base_lines[1].astype(jnp.float32)
    coupling = jnp.sum(adj_lines.astype(jnp.float32) * slope_base, axis=0)
    wall_part = normal_vel[None] * slope_adj + VISCOSITY * curves
    wall_part = wall_part.at[1].add(-coupling)
    wall_part = wall_part.astype(jnp.bfloat16).reshape(comps, cells, part, groups, local_rows)
    wall_part, partial = lax.optimization_barrier((wall_part, partial))
    wall_part = lax.all_to_all(wall_part, "gy", split_axis=3, concat_axis=2, tiled=True)
    wall_part = wall_part.reshape(comps, cells, spanwise, local_rows).astype(jnp.float32)

    partial = boundary_update(base_flow, adjoint, tails, heads, partial)
    partial = side_update(base_flow, adjoint, side_halo, far_side, partial)
    updated = partial + STEP_WEIGHT * wall_part
    wall_index = lax.axis_index("gy") * local_rows + jnp.arange(local_rows, dtype=jnp.int32)
    interior = (wall_index > 0) & (wall_index < total_rows - 1)
    return jnp.where(interior, updated, jnp.float32(0.0))


def far_plan(links):
    count = lax.axis_size("gx")
    tail_senders = {i for i in links}
    head_senders = {(i + 1) % count for i in links}
    assert not (tail_senders & head_senders)
    pairs = [(i, (i + 1) % count) for i in links] + [((i + 1) % count, i) for i in links]
    position = lax.axis_index("gx")
    sends_tail = jnp.zeros((), jnp.bool_)
    gets_tail = jnp.zeros((), jnp.bool_)
    for i in links:
        sends_tail = sends_tail | (position == i)
        gets_tail = gets_tail | (position == (i + 1) % count)
    return pairs, sends_tail, gets_tail


def far_links(mesh):
    devices = mesh.devices
    count = devices.shape[0]
    return tuple(
        bool(devices[i, 0].coords[1] != devices[(i + 1) % count, 0].coords[1]) for i in range(count)
    )


def solution(mesh):
    return jax.shard_map(
        functools.partial(body, far=far_links(mesh)),
        mesh=mesh,
        in_specs=(P(None, "gx", None, "gy"), P(None, "gx", None, "gy"), P(), P()),
        out_specs=P(None, "gx", None, "gy"),
        check_vma=False,
    )
```

```python
import functools

import jax
import jax.numpy as jnp
from jax import lax
from jax.experimental import pallas as pl
from jax.experimental.pallas import tpu as pltpu
from jax.sharding import PartitionSpec as P

C_FIRST = (0.8, -0.2, 4.0 / 105.0, -1.0 / 280.0)
C_SECOND = (1.6, -0.2, 8.0 / 315.0, -1.0 / 560.0)
C_CENTER = -205.0 / 72.0
VISCOSITY = 0.1
STEP_WEIGHT = 0.5
HALO = 4
LANES = 128


def ring_shift(value, axis, forward, far, want_far):
    count = lax.axis_size(axis)
    links = [i for i in range(count) if far[i] == want_far]
    if forward:
        pairs = [(i, (i + 1) % count) for i in links]
    else:
        pairs = [((i + 1) % count, i) for i in links]
    return lax.ppermute(value, axis, pairs)


def cell_update(load, x, write):
    span = load(0, 0, x).shape[0]

    def zshift(v, k):
        return pltpu.roll(v, (span - k) % span, 0)

    def derivs(field, c, second):
        center = load(field, c, x)
        plus = [load(field, c, x + k) for k in range(1, 5)]
        minus = [load(field, c, x - k) for k in range(1, 5)]
        zp = [zshift(center, k) for k in range(1, 5)]
        zm = [zshift(center, span - k) for k in range(1, 5)]
        dx = C_FIRST[0] * (plus[0] - minus[0])
        dz = C_FIRST[0] * (zp[0] - zm[0])
        for k in range(1, 4):
            dx = dx + C_FIRST[k] * (plus[k] - minus[k])
            dz = dz + C_FIRST[k] * (zp[k] - zm[k])
        if not second:
            return center, dx, dz, None, None
        dxx = C_CENTER * center
        dzz = C_CENTER * center
        for k in range(4):
            dxx = dxx + C_SECOND[k] * (plus[k] + minus[k])
            dzz = dzz + C_SECOND[k] * (zp[k] + zm[k])
        return center, dx, dz, dxx, dzz

    base = [derivs(0, j, False) for j in range(3)]
    adj = [derivs(1, c, True) for c in range(3)]
    first_coupling = adj[0][0] * base[0][1] + adj[1][0] * base[1][1] + adj[2][0] * base[2][1]
    last_coupling = adj[0][0] * base[0][2] + adj[1][0] * base[1][2] + adj[2][0] * base[2][2]
    for c in range(3):
        center, dx, dz, dxx, dzz = adj[c]
        tendency = base[0][0] * dx + base[2][0] * dz + VISCOSITY * (dxx + dzz)
        if c == 0:
            tendency = tendency - first_coupling
        elif c == 2:
            tendency = tendency - last_coupling
        write(c, center + STEP_WEIGHT * tendency)


def interior_kernel(base_ref, adj_ref, out_ref):
    first = (pl.program_id(1) + 1) * HALO

    def load(field, c, x):
        return (base_ref if field == 0 else adj_ref)[c, x]

    def step(i, carry):
        def write(c, value):
            out_ref[c, i] = value

        cell_update(load, first + i, write)
        return carry

    lax.fori_loop(0, HALO, step, 0)


def interior_update(base_flow, adjoint):
    comps, cells, span, rows = base_flow.shape
    field_spec = pl.BlockSpec((comps, cells, span, LANES), lambda j, b: (0, 0, 0, j))
    out_spec = pl.BlockSpec((comps, HALO, span, LANES), lambda j, b: (0, b + 1, 0, j))
    return pl.pallas_call(
        interior_kernel,
        grid=(rows // LANES, cells // HALO - 2),
        in_specs=[field_spec, field_spec],
        out_specs=out_spec,
        out_shape=jax.ShapeDtypeStruct(base_flow.shape, jnp.float32),
    )(base_flow, adjoint)


def boundary_kernel(base_ref, adj_ref, tail_ref, head_ref, prev_ref, out_ref, ext_ref):
    comps, cells, span, rows = base_ref.shape
    side = pl.program_id(0)

    @pl.when(side == 0)
    def _():
        ext_ref[0, :, HALO : HALO + cells] = base_ref[...]
        ext_ref[1, :, HALO : HALO + cells] = adj_ref[...]
        ext_ref[:, :, :HALO] = tail_ref[...]
        ext_ref[:, :, HALO + cells :] = head_ref[...]

    first = side * (cells - HALO)
    for lane in range(rows // LANES):
        lanes = pl.ds(lane * LANES, LANES)

        def load(field, c, x, lanes=lanes):
            return ext_ref[field, c, x + HALO, :, lanes]

        def step(i, carry, lanes=lanes, load=load):
            def write(c, value):
                out_ref[c, i, :, lanes] = value

            cell_update(load, first + i, write)
            return carry

        lax.fori_loop(0, HALO, step, 0)


def boundary_update(base_flow, adjoint, tails, heads, previous):
    comps, cells, span, rows = base_flow.shape
    full_spec = pl.BlockSpec((comps, cells, span, rows), lambda s: (0, 0, 0, 0))
    halo_spec = pl.BlockSpec((2, comps, HALO, span, rows), lambda s: (0, 0, 0, 0, 0))
    out_spec = pl.BlockSpec((comps, HALO, span, rows), lambda s: (0, s * (cells // HALO - 1), 0, 0))
    return pl.pallas_call(
        boundary_kernel,
        grid=(2,),
        in_specs=[full_spec, full_spec, halo_spec, halo_spec, pl.BlockSpec(memory_space=pl.ANY)],
        out_specs=out_spec,
        out_shape=jax.ShapeDtypeStruct(base_flow.shape, jnp.float32),
        scratch_shapes=[pltpu.VMEM((2, comps, cells + 2 * HALO, span, rows), jnp.float32)],
        input_output_aliases={4: 0},
    )(base_flow, adjoint, tails, heads, previous)


def side_kernel(side_ref, base_ref, adj_ref, halo_ref, prev_ref, out_ref, ext_ref):
    comps, near, span, rows = base_ref.shape

    @pl.when(side_ref[0] == 0)
    def _():
        ext_ref[:, :, :HALO] = halo_ref[...]
        ext_ref[0, :, HALO:] = base_ref[...]
        ext_ref[1, :, HALO:] = adj_ref[...]

    @pl.when(side_ref[0] != 0)
    def _():
        ext_ref[0, :, :near] = base_ref[...]
        ext_ref[1, :, :near] = adj_ref[...]
        ext_ref[:, :, near:] = halo_ref[...]

    for lane in range(rows // LANES):
        lanes = pl.ds(lane * LANES, LANES)

        def load(field, c, x, lanes=lanes):
            return ext_ref[field, c, x, :, lanes]

        def step(i, carry, lanes=lanes, load=load):
            def write(c, value):
                out_ref[c, i, :, lanes] = value

            cell_update(load, HALO + i, write)
            return carry

        lax.fori_loop(0, HALO, step, 0)


def side_update(base_flow, adjoint, halo, side, previous):
    comps, cells, span, rows = base_flow.shape
    near = 2 * HALO
    last = cells // near - 1
    body_spec = pl.BlockSpec((comps, near, span, rows), lambda i, side_ref: (0, side_ref[0] * last, 0, 0))
    halo_spec = pl.BlockSpec((2, comps, HALO, span, rows), lambda i, side_ref: (0, 0, 0, 0, 0))
    out_spec = pl.BlockSpec(
        (comps, HALO, span, rows), lambda i, side_ref: (0, side_ref[0] * (cells // HALO - 1), 0, 0)
    )
    grid_spec = pltpu.PrefetchScalarGridSpec(
        num_scalar_prefetch=1,
        grid=(1,),
        in_specs=[body_spec, body_spec, halo_spec, pl.BlockSpec(memory_space=pl.ANY)],
        out_specs=out_spec,
        scratch_shapes=[pltpu.VMEM((2, comps, near + HALO, span, rows), jnp.float32)],
    )
    return pl.pallas_call(
        side_kernel,
        grid_spec=grid_spec,
        out_shape=jax.ShapeDtypeStruct(base_flow.shape, jnp.float32),
        input_output_aliases={4: 0},
    )(side, base_flow, adjoint, halo, previous)


def body(base_flow, adjoint, first_op, second_op, far=()):
    comps, cells, spanwise, local_rows = base_flow.shape
    groups = lax.axis_size("gy")
    total_rows = local_rows * groups
    part = spanwise // groups

    low = jnp.concatenate((base_flow, adjoint), 0).astype(jnp.bfloat16)
    low = low.reshape(2 * comps, cells, spanwise, 1, local_rows)
    lines = lax.all_to_all(low, "gy", split_axis=2, concat_axis=3, tiled=True)
    tail_cells = jnp.stack((base_flow[:, cells - HALO :], adjoint[:, cells - HALO :]), 0)
    head_cells = jnp.stack((base_flow[:, :HALO], adjoint[:, :HALO]), 0)
    tails = ring_shift(tail_cells, "gx", True, far, False)
    heads = ring_shift(head_cells, "gx", False, far, False)
    far_pairs, sends_tail, gets_tail = far_plan(far)
    far_send = jnp.where(sends_tail, tail_cells, head_cells)
    partial = interior_update(base_flow, adjoint)
    lines, partial, tails, heads, far_send = lax.optimization_barrier((lines, partial, tails, heads, far_send))
    received = lax.ppermute(far_send, "gx", far_pairs)
    far_side = jnp.where(sends_tail, 1, 0).astype(jnp.int32).reshape(1)
    side_halo = jnp.where(gets_tail | sends_tail, received, tails)
    lines = lines.reshape(2 * comps, cells, part, total_rows)
    base_lines = lines[:comps]
    adj_lines = lines[comps:]
    slope_base = jnp.einsum("fxzk,ik->fxzi", base_lines, first_op, preferred_element_type=jnp.float32)
    slope_adj = jnp.einsum("fxzk,ik->fxzi", adj_lines, first_op, preferred_element_type=jnp.float32)
    curves = jnp.einsum("fxzk,ik->fxzi", adj_lines, second_op, preferred_element_type=jnp.float32)
    normal_vel = base_lines[1].astype(jnp.float32)
    coupling = jnp.sum(adj_lines.astype(jnp.float32) * slope_base, axis=0)
    wall_part = normal_vel[None] * slope_adj + VISCOSITY * curves
    wall_part = wall_part.at[1].add(-coupling)
    wall_part = wall_part.astype(jnp.bfloat16).reshape(comps, cells, part, groups, local_rows)
    wall_part, partial = lax.optimization_barrier((wall_part, partial))
    wall_part = lax.all_to_all(wall_part, "gy", split_axis=3, concat_axis=2, tiled=True)
    wall_part = wall_part.reshape(comps, cells, spanwise, local_rows).astype(jnp.float32)

    partial = boundary_update(base_flow, adjoint, tails, heads, partial)
    partial = side_update(base_flow, adjoint, side_halo, far_side, partial)
    updated = partial + STEP_WEIGHT * wall_part
    wall_index = lax.axis_index("gy") * local_rows + jnp.arange(local_rows, dtype=jnp.int32)
    interior = (wall_index > 0) & (wall_index < total_rows - 1)
    return jnp.where(interior, updated, jnp.float32(0.0))


def far_plan(far):
    count = lax.axis_size("gx")
    links = [i for i in range(count) if far[i]]
    tail_senders = {i for i in links}
    head_senders = {(i + 1) % count for i in links}
    assert links and not (tail_senders & head_senders)
    pairs = [(i, (i + 1) % count) for i in links] + [((i + 1) % count, i) for i in links]
    position = lax.axis_index("gx")
    sends_tail = jnp.zeros((), jnp.bool_)
    gets_tail = jnp.zeros((), jnp.bool_)
    for i in links:
        sends_tail = sends_tail | (position == i)
        gets_tail = gets_tail | (position == (i + 1) % count)
    return pairs, sends_tail, gets_tail


def far_links(mesh):
    devices = mesh.devices
    count = devices.shape[0]
    return tuple(
        bool(devices[i, 0].coords[1] != devices[(i + 1) % count, 0].coords[1]) for i in range(count)
    )


def solution(mesh):
    return jax.shard_map(
        functools.partial(body, far=far_links(mesh)),
        mesh=mesh,
        in_specs=(P(None, "gx", None, "gy"), P(None, "gx", None, "gy"), P(), P()),
        out_specs=P(None, "gx", None, "gy"),
        check_vma=False,
    )
```
